32 devices in a mesh: parts: 2 (over y), cols: 4 (over z), rows: 2 (over x), rep: 2 (over core).
Axes of the slice: x: 2, y: 2, z: 4, core: 2. Of those that a mesh axis runs over, the one named last changes fastest.
Arguments:
- sources: float32 [4096, 64], P(('parts', 'rows')), parts along dimension 0, may hold values from -11 to 11
- source_mass: float32 [4096], P(('parts', 'rows')), parts along dimension 0, may hold values from 0.2 to 5
- targets: float32 [4096, 64], P(('parts', 'cols', 'rep')), parts along dimension 0, may hold values from -6 to 6
- target_mass: float32 [4096], P(('parts', 'cols', 'rep')), parts along dimension 0, may hold values from 0.2 to 5
- fate_panel: float32 [4096, 64], P(('parts', 'cols', 'rep')), parts along dimension 0, may hold values from 0 to 1
Outputs:
- f_pot: float32 [4096], P(('parts', 'rows')), parts along dimension 0
- g_pot: float32 [4096], P(('parts', 'cols', 'rep')), parts along dimension 0
- fate_rows: float32 [4096, 64], P(('parts', 'rows', 'cols', 'rep')), parts along dimension 0
The draws below stay inside these ranges and needn't reach their ends.
There are 2 independent parts, one for each index of `parts`. The reference program is written for one: setup_inputs(seed, part) draws one part's arguments, and reference() takes and returns one part's arrays. A program takes and returns all parts, laid end to end along the dimension named above; each array names one. Nothing has to cross between parts.
All inputs are finite; a program needn't handle non-finite values.
Results may differ from the reference program's by a relative error of at most 0.0003.
Values sent between devices are 32-bit elements; how exact they have to be, the bound alone decides.
No kernel may reach another device: no remote copies, remote signals or barrier semaphores. Data moves between devices by JAX's collectives and lax.ppermute only.
A program may use at most 64 MiB of HBM per device.

```python
import math
import jax
import jax.numpy as jnp
from jax import lax

DIM = 64
FATES = 64
ITERS = 8
NS = 2048
NT = 2048


def draw_sources(key, part):
    key_base = jax.random.fold_in(key, 0)
    return jnp.clip(jax.random.normal(key_base, (NS, DIM), jnp.float32), -6.0, 6.0)


def level_of(rng, shape, pieces, smallest, largest):
    gain = 1.0
    for position, shards_of in pieces:
        draws = jax.random.uniform(jax.random.fold_in(jax.random.fold_in(rng, 6), position), (shards_of,), jnp.float32, smallest / len(pieces), largest / len(pieces))
        gain = gain * jnp.repeat(jnp.exp(draws), shape[position] // shards_of).reshape((-1,) + (1,) * (len(shape) - 1 - position))
    return gain


def centred(key, shape, scale, reach, cuts=(), kind=jnp.bfloat16):
    result = jax.random.normal(key, shape, jnp.float32) * scale
    if len(cuts) > 0:
        result = level_of(key, shape, cuts, -0.22, 0.18) * result
    return jnp.clip(result, min=-reach, max=reach).astype(kind)


def setup_inputs(seed: int = 0, part: int = 0) -> dict:
    key_of = jax.random.split(jax.random.key(seed), 6)
    part_splits = jax.random.split(jax.random.fold_in(key_of[5], part), 6)
    return {
        "sources": draw_sources(jax.random.fold_in(jax.random.fold_in(key_of[5], part), 71), part),
        "source_mass": jnp.clip(jnp.exp(math.log(5.0) - 3.218876 * jax.random.uniform(part_splits[1], (NS,), jnp.float32) ** level_of(part_splits[1], (NS,), ((0, 2),), -0.2, 0.2)), 0.2, 5.0),
        "targets": centred(part_splits[2], (NT, DIM), 1.0, 6.0, ((0, 8),), jnp.float32),
        "target_mass": jnp.clip(jnp.exp(math.log(5.0) - 3.218876 * jax.random.uniform(part_splits[3], (NT,), jnp.float32) ** level_of(part_splits[3], (NT,), ((0, 8),), -0.2, 0.2)), 0.2, 5.0),
        "fate_panel": jnp.clip(1.0 * jax.random.uniform(part_splits[4], (NT, FATES), jnp.float32) ** level_of(part_splits[4], (NT, FATES), ((0, 8),), -0.2, 0.2), 0.0, 1.0),
    }


entropic = 0.1
relaxed = 1.0 / 1.1


def pair_cost(lhs_rows, rhs_rows):
    lhs_sq = jnp.sum(lhs_rows * lhs_rows, axis=1)
    rhs_sq = jnp.sum(rhs_rows * rhs_rows, axis=1)
    products = lax.dot_general(lhs_rows, rhs_rows, (((1,), (1,)), ((), ())), precision=lax.Precision.HIGHEST, preferred_element_type=jnp.float32)
    return (lhs_sq[:, None] + rhs_sq[None, :] - 2.0 * products) / DIM


def reference(sources, source_mass, targets, target_mass, fate_panel):
    log_a = jnp.log(source_mass / NS)
    log_b = jnp.log(target_mass / NT)
    row_size = math.gcd(NS, 512)
    col_size = math.gcd(NT, 512)
    src_blocks = sources.reshape(NS // row_size, row_size, DIM)
    tgt_blocks = targets.reshape(NT // col_size, col_size, DIM)

    def row_lse(g_pot):
        def single_block(src_block):
            scores = log_b[None, :] + (g_pot[None, :] - pair_cost(src_block, targets)) / entropic
            highest = jnp.max(scores, axis=1)
            totals = jnp.sum(jnp.exp(scores - highest[:, None]), axis=1)
            return -relaxed * entropic * (highest + jnp.log(totals))
        return lax.map(single_block, src_blocks).reshape(NS)

    def col_lse(f_pot):
        def single_block(tgt_block):
            scores = log_a[:, None] + (f_pot[:, None] - pair_cost(sources, tgt_block)) / entropic
            highest = jnp.max(scores, axis=0)
            totals = jnp.sum(jnp.exp(scores - highest[None, :]), axis=0)
            return -relaxed * entropic * (highest + jnp.log(totals))
        return lax.map(single_block, tgt_blocks).reshape(NT)

    g_pot = jnp.zeros((NT,), jnp.float32)
    f_pot = jnp.zeros((NS,), jnp.float32)
    for iteration in range(ITERS):
        f_pot = row_lse(g_pot)
        g_pot = col_lse(f_pot)

    def fate_block(src_block):
        scores = log_b[None, :] + (g_pot[None, :] - pair_cost(src_block, targets)) / entropic
        highest = jnp.max(scores, axis=1)
        weights = jnp.exp(scores - highest[:, None])
        totals = jnp.sum(weights, axis=1)
        weighted = jnp.dot(weights, fate_panel, precision=lax.Precision.HIGHEST, preferred_element_type=jnp.float32)
        return weighted / totals[:, None]

    fate_rows = lax.map(fate_block, src_blocks).reshape(NS, FATES)
    return (f_pot, g_pot, fate_rows)
```

```python
import jax
import jax.numpy as jnp
from jax import lax
from jax.sharding import PartitionSpec as P

ITERS = 8


entropic = 0.1
relaxed = 1.0 / 1.1


def pair_cost(lhs_rows, lhs_sq, rhs_rows, rhs_sq):
    products = lax.dot_general(
        lhs_rows,
        rhs_rows,
        (((1,), (1,)), ((), ())),
        precision=lax.Precision.HIGHEST,
        preferred_element_type=jnp.float32,
    )
    return (lhs_sq[:, None] + rhs_sq[None, :] - 2.0 * products) / lhs_rows.shape[1]


def is_pow2(n):
    return n > 0 and (n & (n - 1)) == 0


def merge(m_one, s_one, m_two, s_two):
    top = jnp.maximum(m_one, m_two)
    return top, s_one * jnp.exp(m_one - top) + s_two * jnp.exp(m_two - top)


def lse_allreduce(maxima, totals, axes):
    if not all(is_pow2(lax.axis_size(name)) for name in axes):
        peak = lax.pmax(maxima, axes)
        return peak, lax.psum(totals * jnp.exp(maxima - peak), axes)
    for name in axes:
        size = lax.axis_size(name)
        index = lax.axis_index(name)
        step = 1
        while step < size:
            perm = [(i, i ^ step) for i in range(size)]
            other = lax.ppermute(jnp.stack([maxima, totals]), name, perm)
            other_m, other_s = other[0], other[1]
            low = (index & step) == 0
            lo_m = jnp.where(low, maxima, other_m)
            hi_m = jnp.where(low, other_m, maxima)
            lo_s = jnp.where(low, totals, other_s)
            hi_s = jnp.where(low, other_s, totals)
            maxima, totals = merge(lo_m, lo_s, hi_m, hi_s)
            step *= 2
    return maxima, totals


def lse_halving(maxima, totals, weighted, dims):
    for name, step in dims:
        size = lax.axis_size(name)
        perm = [(i, i ^ step) for i in range(size)]
        high = (lax.axis_index(name) & step) != 0

        def split(x):
            lower = lax.index_in_dim(x, 0, axis=0, keepdims=False)
            upper = lax.index_in_dim(x, 1, axis=0, keepdims=False)
            return jnp.where(high, upper, lower), jnp.where(high, lower, upper)

        keep_m, send_m = split(maxima)
        keep_s, send_s = split(totals)
        keep_w, send_w = split(weighted)
        packed = jnp.concatenate([send_w, send_m[..., None], send_s[..., None]], axis=-1)
        packed = lax.ppermute(packed, name, perm)
        fates = weighted.shape[-1]
        recv_w, recv_m, recv_s = packed[..., :fates], packed[..., fates], packed[..., fates + 1]
        top = jnp.maximum(keep_m, recv_m)
        keep_f = jnp.exp(keep_m - top)
        recv_f = jnp.exp(recv_m - top)
        maxima = top
        totals = keep_s * keep_f + recv_s * recv_f
        weighted = keep_w * keep_f[..., None] + recv_w * recv_f[..., None]
    return maxima, totals, weighted


def body(sources, source_mass, targets, target_mass, fate_panel):
    src_count = sources.shape[0]
    tgt_count = targets.shape[0]
    all_sources = src_count * lax.axis_size("rows")
    all_targets = tgt_count * lax.axis_size(("cols", "rep"))
    log_a = jnp.log(source_mass / all_sources)
    log_b = jnp.log(target_mass / all_targets)
    src_sq = jnp.sum(sources * sources, axis=1)
    tgt_sq = jnp.sum(targets * targets, axis=1)
    cost = pair_cost(sources, src_sq, targets, tgt_sq)

    g_pot = jnp.zeros((tgt_count,), jnp.float32)
    f_pot = jnp.zeros((src_count,), jnp.float32)
    for iteration in range(ITERS):
        scores = log_b[None, :] + (g_pot[None, :] - cost) / entropic
        maxima = jnp.max(scores, axis=1)
        totals = jnp.sum(jnp.exp(scores - maxima[:, None]), axis=1)
        peak, whole = lse_allreduce(maxima, totals, ("rep", "cols"))
        f_pot = -relaxed * entropic * (peak + jnp.log(whole))

        scores = log_a[:, None] + (f_pot[:, None] - cost) / entropic
        maxima = jnp.max(scores, axis=0)
        totals = jnp.sum(jnp.exp(scores - maxima[None, :]), axis=0)
        peak, whole = lse_allreduce(maxima, totals, ("rows",))
        g_pot = -relaxed * entropic * (peak + jnp.log(whole))

    scores = log_b[None, :] + (g_pot[None, :] - cost) / entropic
    maxima = jnp.max(scores, axis=1)
    weights = jnp.exp(scores - maxima[:, None])
    totals = jnp.sum(weights, axis=1)
    weighted = jnp.dot(
        weights, fate_panel, precision=lax.Precision.HIGHEST, preferred_element_type=jnp.float32
    )

    col_size = lax.axis_size("cols")
    rep_size = lax.axis_size("rep")
    fates = fate_panel.shape[1]
    if is_pow2(col_size) and is_pow2(rep_size):
        col_bits = col_size.bit_length() - 1
        rep_bits = rep_size.bit_length() - 1
        lead = (2,) * (col_bits + rep_bits)
        block = src_count // (col_size * rep_size)
        maxima = maxima.reshape(lead + (block,))
        totals = totals.reshape(lead + (block,))
        weighted = weighted.reshape(lead + (block, fates))
        order = [("cols", 1 << b) for b in range(col_bits - 1, -1, -1)]
        order += [("rep", 1 << b) for b in range(rep_bits - 1, -1, -1)]
        plan = list(range(len(order) - 1, col_bits - 1, -1)) + list(range(col_bits - 1, -1, -1))
        perm_dims = plan + list(range(len(order), len(order) + 1))
        maxima = jnp.transpose(maxima, perm_dims)
        totals = jnp.transpose(totals, perm_dims)
        weighted = jnp.transpose(weighted, perm_dims + [len(order) + 1])
        maxima, totals, weighted = lse_halving(
            maxima, totals, weighted, [order[d] for d in plan]
        )
        fate_rows = weighted / totals[:, None]
    else:
        whole_peak = lax.pmax(maxima, ("cols", "rep"))
        factor = jnp.exp(maxima - whole_peak)
        part_weighted, part_total = (
            lax.psum_scatter(
                weighted * factor[:, None], ("cols", "rep"), scatter_dimension=0, tiled=True
            ),
            lax.psum_scatter(totals * factor, ("cols", "rep"), scatter_dimension=0, tiled=True),
        )
        fate_rows = part_weighted / part_total[:, None]
    return (f_pot, g_pot, fate_rows)


def solution(mesh):
    in_specs = (
        P(("parts", "rows"), None),
        P(("parts", "rows")),
        P(("parts", "cols", "rep"), None),
        P(("parts", "cols", "rep")),
        P(("parts", "cols", "rep"), None),
    )
    out_specs = (
        P(("parts", "rows")),
        P(("parts", "cols", "rep")),
        P(("parts", "rows", "cols", "rep"), None),
    )
    return jax.shard_map(body, mesh=mesh, in_specs=in_specs, out_specs=out_specs, check_vma=False)
```

```python
import jax
import jax.numpy as jnp
from jax import lax
from jax.sharding import PartitionSpec as P

ITERS = 8


entropic = 0.1
relaxed = 1.0 / 1.1


def pair_cost(lhs_rows, lhs_sq, rhs_rows, rhs_sq):
    products = lax.dot_general(
        lhs_rows,
        rhs_rows,
        (((1,), (1,)), ((), ())),
        precision=lax.Precision.HIGHEST,
        preferred_element_type=jnp.float32,
    )
    return (lhs_sq[:, None] + rhs_sq[None, :] - 2.0 * products) / lhs_rows.shape[1]


def is_pow2(n):
    return n > 0 and (n & (n - 1)) == 0


def merge(m_one, s_one, m_two, s_two):
    top = jnp.maximum(m_one, m_two)
    return top, s_one * jnp.exp(m_one - top) + s_two * jnp.exp(m_two - top)


def lse_allreduce(maxima, totals, axes):
    if not all(is_pow2(lax.axis_size(name)) for name in axes):
        peak = lax.pmax(maxima, axes)
        return peak, lax.psum(totals * jnp.exp(maxima - peak), axes)
    for name in axes:
        size = lax.axis_size(name)
        index = lax.axis_index(name)
        step = 1
        while step < size:
            perm = [(i, i ^ step) for i in range(size)]
            other = lax.ppermute(jnp.stack([maxima, totals]), name, perm)
            other_m, other_s = other[0], other[1]
            low = (index & step) == 0
            lo_m = jnp.where(low, maxima, other_m)
            hi_m = jnp.where(low, other_m, maxima)
            lo_s = jnp.where(low, totals, other_s)
            hi_s = jnp.where(low, other_s, totals)
            maxima, totals = merge(lo_m, lo_s, hi_m, hi_s)
            step *= 2
    return maxima, totals


def lse_exchange(maxima, totals, axes):
    size = lax.axis_size(axes)
    index = lax.axis_index(axes)
    payload = jnp.stack([maxima, totals])
    received = [payload]
    for shift in range(1, size):
        perm = [(i, (i + shift) % size) for i in range(size)]
        received.append(lax.ppermute(payload, axes, perm))
    received = jnp.stack(received)
    ordered = [
        lax.dynamic_index_in_dim(received, (index - rank) % size, axis=0, keepdims=False)
        for rank in range(size)
    ]
    peak = ordered[0][0]
    for item in ordered[1:]:
        peak = jnp.maximum(peak, item[0])
    whole = ordered[0][1] * jnp.exp(ordered[0][0] - peak)
    for item in ordered[1:]:
        whole = whole + item[1] * jnp.exp(item[0] - peak)
    return peak, whole


def lse_halving(maxima, totals, weighted, dims):
    for name, step in dims:
        size = lax.axis_size(name)
        perm = [(i, i ^ step) for i in range(size)]
        high = (lax.axis_index(name) & step) != 0

        def split(x):
            lower = lax.index_in_dim(x, 0, axis=0, keepdims=False)
            upper = lax.index_in_dim(x, 1, axis=0, keepdims=False)
            return jnp.where(high, upper, lower), jnp.where(high, lower, upper)

        keep_m, send_m = split(maxima)
        keep_s, send_s = split(totals)
        keep_w, send_w = split(weighted)
        packed = jnp.concatenate([send_w, send_m[..., None], send_s[..., None]], axis=-1)
        packed = lax.ppermute(packed, name, perm)
        fates = weighted.shape[-1]
        recv_w, recv_m, recv_s = packed[..., :fates], packed[..., fates], packed[..., fates + 1]
        top = jnp.maximum(keep_m, recv_m)
        keep_f = jnp.exp(keep_m - top)
        recv_f = jnp.exp(recv_m - top)
        maxima = top
        totals = keep_s * keep_f + recv_s * recv_f
        weighted = keep_w * keep_f[..., None] + recv_w * recv_f[..., None]
    return maxima, totals, weighted


def body_split(sources, source_mass, targets, target_mass, fate_panel):
    src_count = sources.shape[0]
    tgt_count = targets.shape[0]
    all_sources = src_count * lax.axis_size("rows")
    all_targets = tgt_count * lax.axis_size(("cols", "rep"))
    log_a = jnp.log(source_mass / all_sources)
    log_b = jnp.log(target_mass / all_targets)
    src_sq = jnp.sum(sources * sources, axis=1)
    tgt_sq = jnp.sum(targets * targets, axis=1)
    cost = pair_cost(sources, src_sq, targets, tgt_sq)

    g_pot = jnp.zeros((tgt_count,), jnp.float32)
    f_pot = jnp.zeros((src_count,), jnp.float32)
    for iteration in range(ITERS):
        scores = log_b[None, :] + (g_pot[None, :] - cost) / entropic
        maxima = jnp.max(scores, axis=1)
        totals = jnp.sum(jnp.exp(scores - maxima[:, None]), axis=1)
        peak, whole = lse_allreduce(maxima, totals, ("rep", "cols"))
        f_pot = -relaxed * entropic * (peak + jnp.log(whole))

        scores = log_a[:, None] + (f_pot[:, None] - cost) / entropic
        maxima = jnp.max(scores, axis=0)
        totals = jnp.sum(jnp.exp(scores - maxima[None, :]), axis=0)
        peak, whole = lse_allreduce(maxima, totals, ("rows",))
        g_pot = -relaxed * entropic * (peak + jnp.log(whole))

    return (f_pot,) + fate_pullback(cost, log_b, g_pot, fate_panel)


def fate_pullback(cost, log_b, g_pot, fate_panel):
    src_count = cost.shape[0]
    scores = log_b[None, :] + (g_pot[None, :] - cost) / entropic
    maxima = jnp.max(scores, axis=1)
    weights = jnp.exp(scores - maxima[:, None])
    totals = jnp.sum(weights, axis=1)
    weighted = jnp.dot(
        weights, fate_panel, precision=lax.Precision.HIGHEST, preferred_element_type=jnp.float32
    )
    col_size = lax.axis_size("cols")
    rep_size = lax.axis_size("rep")
    fates = fate_panel.shape[1]
    if is_pow2(col_size) and is_pow2(rep_size):
        col_bits = col_size.bit_length() - 1
        rep_bits = rep_size.bit_length() - 1
        lead = (2,) * (col_bits + rep_bits)
        block = src_count // (col_size * rep_size)
        maxima = maxima.reshape(lead + (block,))
        totals = totals.reshape(lead + (block,))
        weighted = weighted.reshape(lead + (block, fates))
        order = [("cols", 1 << b) for b in range(col_bits - 1, -1, -1)]
        order += [("rep", 1 << b) for b in range(rep_bits - 1, -1, -1)]
        plan = list(range(len(order) - 1, col_bits - 1, -1)) + list(range(col_bits - 1, -1, -1))
        perm_dims = plan + list(range(len(order), len(order) + 1))
        maxima = jnp.transpose(maxima, perm_dims)
        totals = jnp.transpose(totals, perm_dims)
        weighted = jnp.transpose(weighted, perm_dims + [len(order) + 1])
        maxima, totals, weighted = lse_halving(
            maxima, totals, weighted, [order[d] for d in plan]
        )
        fate_rows = weighted / totals[:, None]
    else:
        whole_peak = lax.pmax(maxima, ("cols", "rep"))
        factor = jnp.exp(maxima - whole_peak)
        part_weighted, part_total = (
            lax.psum_scatter(
                weighted * factor[:, None], ("cols", "rep"), scatter_dimension=0, tiled=True
            ),
            lax.psum_scatter(totals * factor, ("cols", "rep"), scatter_dimension=0, tiled=True),
        )
        fate_rows = part_weighted / part_total[:, None]
    return (g_pot, fate_rows)


ROW_AXES = (("rep",), ("cols",))


def body(sources, source_mass, targets, target_mass, fate_panel):
    row_count = lax.axis_size("rows")
    if row_count != 2 or lax.axis_size("cols") > 8:
        return body_split(sources, source_mass, targets, target_mass, fate_panel)
    src_count = sources.shape[0]
    tgt_count = targets.shape[0]
    row = lax.axis_index("rows")
    mine = jnp.concatenate([sources, source_mass[:, None]], axis=1)
    theirs = lax.ppermute(mine, "rows", [(0, 1), (1, 0)])
    first = jnp.where(row == 0, mine, theirs)
    second = jnp.where(row == 0, theirs, mine)
    gathered = jnp.concatenate([first, second], axis=0)
    all_src = gathered[:, : sources.shape[1]]
    all_mass = gathered[:, sources.shape[1]]
    all_sources = src_count * row_count
    all_targets = tgt_count * lax.axis_size(("cols", "rep"))
    log_a = jnp.log(all_mass / all_sources)
    log_b = jnp.log(target_mass / all_targets)
    src_sq = jnp.sum(all_src * all_src, axis=1)
    tgt_sq = jnp.sum(targets * targets, axis=1)
    cost = pair_cost(all_src, src_sq, targets, tgt_sq)

    g_pot = jnp.zeros((tgt_count,), jnp.float32)
    f_all = jnp.zeros((all_sources,), jnp.float32)
    for iteration in range(ITERS):
        scores = log_b[None, :] + (g_pot[None, :] - cost) / entropic
        maxima = jnp.max(scores, axis=1)
        totals = jnp.sum(jnp.exp(scores - maxima[:, None]), axis=1)
        for axes in ROW_AXES:
            if len(axes) == 1 and lax.axis_size(axes[0]) == 2:
                maxima, totals = lse_allreduce(maxima, totals, axes)
            else:
                maxima, totals = lse_exchange(maxima, totals, axes)
        f_all = -relaxed * entropic * (maxima + jnp.log(totals))

        scores = log_a[:, None] + (f_all[:, None] - cost) / entropic
        maxima = jnp.max(scores, axis=0)
        totals = jnp.sum(jnp.exp(scores - maxima[None, :]), axis=0)
        g_pot = -relaxed * entropic * (maxima + jnp.log(totals))

    f_pot = lax.dynamic_slice_in_dim(f_all, row * src_count, src_count)
    cost_mine = lax.dynamic_slice_in_dim(cost, row * src_count, src_count, axis=0)
    return (f_pot,) + fate_pullback(cost_mine, log_b, g_pot, fate_panel)


def solution(mesh):
    in_specs = (
        P(("parts", "rows"), None),
        P(("parts", "rows")),
        P(("parts", "cols", "rep"), None),
        P(("parts", "cols", "rep")),
        P(("parts", "cols", "rep"), None),
    )
    out_specs = (
        P(("parts", "rows")),
        P(("parts", "cols", "rep")),
        P(("parts", "rows", "cols", "rep"), None),
    )
    return jax.shard_map(body, mesh=mesh, in_specs=in_specs, out_specs=out_specs, check_vma=False)
```

```python
import jax
import jax.numpy as jnp
from jax import lax
from jax.sharding import PartitionSpec as P

ITERS = 8


entropic = 0.1
relaxed = 1.0 / 1.1


def pair_cost(lhs_rows, lhs_sq, rhs_rows, rhs_sq):
    products = lax.dot_general(
        lhs_rows,
        rhs_rows,
        (((1,), (1,)), ((), ())),
        precision=lax.Precision.HIGHEST,
        preferred_element_type=jnp.float32,
    )
    return (lhs_sq[:, None] + rhs_sq[None, :] - 2.0 * products) / lhs_rows.shape[1]


def is_pow2(n):
    return n > 0 and (n & (n - 1)) == 0


def merge(m_one, s_one, m_two, s_two):
    top = jnp.maximum(m_one, m_two)
    return top, s_one * jnp.exp(m_one - top) + s_two * jnp.exp(m_two - top)


def lse_allreduce(maxima, totals, axes):
    if not all(is_pow2(lax.axis_size(name)) for name in axes):
        peak = lax.pmax(maxima, axes)
        return peak, lax.psum(totals * jnp.exp(maxima - peak), axes)
    for name in axes:
        size = lax.axis_size(name)
        index = lax.axis_index(name)
        step = 1
        while step < size:
            perm = [(i, i ^ step) for i in range(size)]
            other = lax.ppermute(jnp.stack([maxima, totals]), name, perm)
            other_m, other_s = other[0], other[1]
            low = (index & step) == 0
            lo_m = jnp.where(low, maxima, other_m)
            hi_m = jnp.where(low, other_m, maxima)
            lo_s = jnp.where(low, totals, other_s)
            hi_s = jnp.where(low, other_s, totals)
            maxima, totals = merge(lo_m, lo_s, hi_m, hi_s)
            step *= 2
    return maxima, totals


def lse_exchange(maxima, totals, axes):
    size = lax.axis_size(axes)
    index = lax.axis_index(axes)
    payload = jnp.stack([maxima, totals])
    received = [payload]
    for shift in range(1, size):
        perm = [(i, (i + shift) % size) for i in range(size)]
        received.append(lax.ppermute(payload, axes, perm))
    received = jnp.stack(received)
    ordered = [
        lax.dynamic_index_in_dim(received, (index - rank) % size, axis=0, keepdims=False)
        for rank in range(size)
    ]
    peak = ordered[0][0]
    for item in ordered[1:]:
        peak = jnp.maximum(peak, item[0])
    whole = ordered[0][1] * jnp.exp(ordered[0][0] - peak)
    for item in ordered[1:]:
        whole = whole + item[1] * jnp.exp(item[0] - peak)
    return peak, whole


def lse_halving(maxima, totals, weighted, dims):
    for name, step in dims:
        size = lax.axis_size(name)
        perm = [(i, i ^ step) for i in range(size)]
        high = (lax.axis_index(name) & step) != 0

        def split(x):
            lower = lax.index_in_dim(x, 0, axis=0, keepdims=False)
            upper = lax.index_in_dim(x, 1, axis=0, keepdims=False)
            return jnp.where(high, upper, lower), jnp.where(high, lower, upper)

        keep_m, send_m = split(maxima)
        keep_s, send_s = split(totals)
        keep_w, send_w = split(weighted)
        packed = jnp.concatenate([send_w, send_m[..., None], send_s[..., None]], axis=-1)
        packed = lax.ppermute(packed, name, perm)
        fates = weighted.shape[-1]
        recv_w, recv_m, recv_s = packed[..., :fates], packed[..., fates], packed[..., fates + 1]
        top = jnp.maximum(keep_m, recv_m)
        keep_f = jnp.exp(keep_m - top)
        recv_f = jnp.exp(recv_m - top)
        maxima = top
        totals = keep_s * keep_f + recv_s * recv_f
        weighted = keep_w * keep_f[..., None] + recv_w * recv_f[..., None]
    return maxima, totals, weighted


def body_split(sources, source_mass, targets, target_mass, fate_panel):
    src_count = sources.shape[0]
    tgt_count = targets.shape[0]
    all_sources = src_count * lax.axis_size("rows")
    all_targets = tgt_count * lax.axis_size(("cols", "rep"))
    log_a = jnp.log(source_mass / all_sources)
    log_b = jnp.log(target_mass / all_targets)
    src_sq = jnp.sum(sources * sources, axis=1)
    tgt_sq = jnp.sum(targets * targets, axis=1)
    cost = pair_cost(sources, src_sq, targets, tgt_sq)

    g_pot = jnp.zeros((tgt_count,), jnp.float32)
    f_pot = jnp.zeros((src_count,), jnp.float32)
    for iteration in range(ITERS):
        scores = log_b[None, :] + (g_pot[None, :] - cost) / entropic
        maxima = jnp.max(scores, axis=1)
        totals = jnp.sum(jnp.exp(scores - maxima[:, None]), axis=1)
        peak, whole = lse_allreduce(maxima, totals, ("rep", "cols"))
        f_pot = -relaxed * entropic * (peak + jnp.log(whole))

        scores = log_a[:, None] + (f_pot[:, None] - cost) / entropic
        maxima = jnp.max(scores, axis=0)
        totals = jnp.sum(jnp.exp(scores - maxima[None, :]), axis=0)
        peak, whole = lse_allreduce(maxima, totals, ("rows",))
        g_pot = -relaxed * entropic * (peak + jnp.log(whole))

    return (f_pot,) + fate_pullback(cost, log_b, g_pot, fate_panel)


def lse_scatter_exchange(maxima, totals, weighted, name):
    size = lax.axis_size(name)
    index = lax.axis_index(name)
    fates = weighted.shape[-1]
    packed = jnp.concatenate([weighted, maxima[..., None], totals[..., None]], axis=-1)
    parts = [lax.dynamic_index_in_dim(packed, index, axis=0, keepdims=False)]
    for shift in range(1, size):
        perm = [(i, (i + shift) % size) for i in range(size)]
        send = lax.dynamic_index_in_dim(packed, (index + shift) % size, axis=0, keepdims=False)
        parts.append(lax.ppermute(send, name, perm))
    top = parts[0][..., fates]
    for part in parts[1:]:
        top = jnp.maximum(top, part[..., fates])
    totals = None
    weighted = None
    for part in parts:
        factor = jnp.exp(part[..., fates] - top)
        add_s = part[..., fates + 1] * factor
        add_w = part[..., :fates] * factor[..., None]
        totals = add_s if totals is None else totals + add_s
        weighted = add_w if weighted is None else weighted + add_w
    return top, totals, weighted


def fate_pullback(cost, log_b, g_pot, fate_panel):
    src_count = cost.shape[0]
    scores = log_b[None, :] + (g_pot[None, :] - cost) / entropic
    maxima = jnp.max(scores, axis=1)
    weights = jnp.exp(scores - maxima[:, None])
    totals = jnp.sum(weights, axis=1)
    weighted = jnp.dot(
        weights, fate_panel, precision=lax.Precision.HIGHEST, preferred_element_type=jnp.float32
    )
    col_size = lax.axis_size("cols")
    rep_size = lax.axis_size("rep")
    fates = fate_panel.shape[1]
    if rep_size == 2 and col_size <= 8:
        block = src_count // (col_size * rep_size)
        maxima = jnp.swapaxes(maxima.reshape(col_size, rep_size, block), 0, 1)
        totals = jnp.swapaxes(totals.reshape(col_size, rep_size, block), 0, 1)
        weighted = jnp.swapaxes(weighted.reshape(col_size, rep_size, block, fates), 0, 1)
        maxima, totals, weighted = lse_halving(maxima, totals, weighted, [("rep", 1)])
        maxima, totals, weighted = lse_scatter_exchange(maxima, totals, weighted, "cols")
        fate_rows = weighted / totals[:, None]
    elif is_pow2(col_size) and is_pow2(rep_size):
        col_bits = col_size.bit_length() - 1
        rep_bits = rep_size.bit_length() - 1
        lead = (2,) * (col_bits + rep_bits)
        block = src_count // (col_size * rep_size)
        maxima = maxima.reshape(lead + (block,))
        totals = totals.reshape(lead + (block,))
        weighted = weighted.reshape(lead + (block, fates))
        order = [("cols", 1 << b) for b in range(col_bits - 1, -1, -1)]
        order += [("rep", 1 << b) for b in range(rep_bits - 1, -1, -1)]
        plan = list(range(len(order) - 1, col_bits - 1, -1)) + list(range(col_bits - 1, -1, -1))
        perm_dims = plan + list(range(len(order), len(order) + 1))
        maxima = jnp.transpose(maxima, perm_dims)
        totals = jnp.transpose(totals, perm_dims)
        weighted = jnp.transpose(weighted, perm_dims + [len(order) + 1])
        maxima, totals, weighted = lse_halving(
            maxima, totals, weighted, [order[d] for d in plan]
        )
        fate_rows = weighted / totals[:, None]
    else:
        whole_peak = lax.pmax(maxima, ("cols", "rep"))
        factor = jnp.exp(maxima - whole_peak)
        part_weighted, part_total = (
            lax.psum_scatter(
                weighted * factor[:, None], ("cols", "rep"), scatter_dimension=0, tiled=True
            ),
            lax.psum_scatter(totals * factor, ("cols", "rep"), scatter_dimension=0, tiled=True),
        )
        fate_rows = part_weighted / part_total[:, None]
    return (g_pot, fate_rows)


ROW_AXES = (("rep",), ("cols",))


def row_reduce(maxima, totals):
    for axes in ROW_AXES:
        if len(axes) == 1 and lax.axis_size(axes[0]) == 2:
            maxima, totals = lse_allreduce(maxima, totals, axes)
        else:
            maxima, totals = lse_exchange(maxima, totals, axes)
    return maxima, totals


def body(sources, source_mass, targets, target_mass, fate_panel):
    row_count = lax.axis_size("rows")
    if row_count != 2 or lax.axis_size("cols") > 8:
        return body_split(sources, source_mass, targets, target_mass, fate_panel)
    src_count = sources.shape[0]
    tgt_count = targets.shape[0]
    dim = sources.shape[1]
    row = lax.axis_index("rows")
    mine = jnp.concatenate([sources.T, source_mass[None, :]], axis=0)
    theirs = lax.ppermute(mine, "rows", [(0, 1), (1, 0)])
    halves = jnp.stack([mine, theirs])
    src_t = halves[:, :dim, :]
    all_mass = halves[:, dim, :]
    all_sources = src_count * row_count
    all_targets = tgt_count * lax.axis_size(("cols", "rep"))
    log_a = jnp.log(all_mass / all_sources)
    log_b = jnp.log(target_mass / all_targets)
    src_sq = jnp.sum(src_t * src_t, axis=1)
    tgt_sq = jnp.sum(targets * targets, axis=1)
    products = lax.dot_general(
        src_t,
        targets,
        (((1,), (1,)), ((), ())),
        precision=lax.Precision.HIGHEST,
        preferred_element_type=jnp.float32,
    )
    cost = (src_sq[:, :, None] + tgt_sq[None, None, :] - 2.0 * products) / dim

    first = row == 0
    g_pot = jnp.zeros((tgt_count,), jnp.float32)
    for iteration in range(ITERS):
        scores = log_b[None, None, :] + (g_pot[None, None, :] - cost) / entropic
        maxima = jnp.max(scores, axis=2)
        totals = jnp.sum(jnp.exp(scores - maxima[:, :, None]), axis=2)
        maxima, totals = row_reduce(maxima, totals)
        f_both = -relaxed * entropic * (maxima + jnp.log(totals))

        scores = log_a[:, :, None] + (f_both[:, :, None] - cost) / entropic
        maxima = jnp.max(scores, axis=1)
        totals = jnp.sum(jnp.exp(scores - maxima[:, None, :]), axis=1)
        lo_m = jnp.where(first, maxima[0], maxima[1])
        hi_m = jnp.where(first, maxima[1], maxima[0])
        lo_s = jnp.where(first, totals[0], totals[1])
        hi_s = jnp.where(first, totals[1], totals[0])
        maxima, totals = merge(lo_m, lo_s, hi_m, hi_s)
        g_pot = -relaxed * entropic * (maxima + jnp.log(totals))

    return (f_both[0],) + fate_pullback(cost[0], log_b, g_pot, fate_panel)


def solution(mesh):
    in_specs = (
        P(("parts", "rows"), None),
        P(("parts", "rows")),
        P(("parts", "cols", "rep"), None),
        P(("parts", "cols", "rep")),
        P(("parts", "cols", "rep"), None),
    )
    out_specs = (
        P(("parts", "rows")),
        P(("parts", "cols", "rep")),
        P(("parts", "rows", "cols", "rep"), None),
    )
    return jax.shard_map(body, mesh=mesh, in_specs=in_specs, out_specs=out_specs, check_vma=False)
```

```python
import jax
import jax.numpy as jnp
from jax import lax
from jax.sharding import PartitionSpec as P

ITERS = 8


entropic = 0.1
relaxed = 1.0 / 1.1


def pair_cost(lhs_rows, lhs_sq, rhs_rows, rhs_sq):
    products = lax.dot_general(
        lhs_rows,
        rhs_rows,
        (((1,), (1,)), ((), ())),
        precision=lax.Precision.HIGHEST,
        preferred_element_type=jnp.float32,
    )
    return (lhs_sq[:, None] + rhs_sq[None, :] - 2.0 * products) / lhs_rows.shape[1]


def is_pow2(n):
    return n > 0 and (n & (n - 1)) == 0


def merge(m_one, s_one, m_two, s_two):
    top = jnp.maximum(m_one, m_two)
    return top, s_one * jnp.exp(m_one - top) + s_two * jnp.exp(m_two - top)


def lse_allreduce(maxima, totals, axes):
    if not all(is_pow2(lax.axis_size(name)) for name in axes):
        peak = lax.pmax(maxima, axes)
        return peak, lax.psum(totals * jnp.exp(maxima - peak), axes)
    for name in axes:
        size = lax.axis_size(name)
        index = lax.axis_index(name)
        step = 1
        while step < size:
            perm = [(i, i ^ step) for i in range(size)]
            other = lax.ppermute(jnp.stack([maxima, totals]), name, perm)
            other_m, other_s = other[0], other[1]
            low = (index & step) == 0
            lo_m = jnp.where(low, maxima, other_m)
            hi_m = jnp.where(low, other_m, maxima)
            lo_s = jnp.where(low, totals, other_s)
            hi_s = jnp.where(low, other_s, totals)
            maxima, totals = merge(lo_m, lo_s, hi_m, hi_s)
            step *= 2
    return maxima, totals


def lse_exchange(maxima, totals, axes):
    size = lax.axis_size(axes)
    index = lax.axis_index(axes)
    payload = jnp.stack([maxima, totals])
    received = [payload]
    for shift in range(1, size):
        perm = [(i, (i + shift) % size) for i in range(size)]
        received.append(lax.ppermute(payload, axes, perm))
    received = jnp.stack(received)
    ordered = [
        lax.dynamic_index_in_dim(received, (index - rank) % size, axis=0, keepdims=False)
        for rank in range(size)
    ]
    peak = ordered[0][0]
    for item in ordered[1:]:
        peak = jnp.maximum(peak, item[0])
    whole = ordered[0][1] * jnp.exp(ordered[0][0] - peak)
    for item in ordered[1:]:
        whole = whole + item[1] * jnp.exp(item[0] - peak)
    return peak, whole


def lse_halving(maxima, totals, weighted, dims):
    for name, step in dims:
        size = lax.axis_size(name)
        perm = [(i, i ^ step) for i in range(size)]
        high = (lax.axis_index(name) & step) != 0

        def split(x):
            lower = lax.index_in_dim(x, 0, axis=0, keepdims=False)
            upper = lax.index_in_dim(x, 1, axis=0, keepdims=False)
            return jnp.where(high, upper, lower), jnp.where(high, lower, upper)

        keep_m, send_m = split(maxima)
        keep_s, send_s = split(totals)
        keep_w, send_w = split(weighted)
        packed = jnp.concatenate([send_w, send_m[..., None], send_s[..., None]], axis=-1)
        packed = lax.ppermute(packed, name, perm)
        fates = weighted.shape[-1]
        recv_w, recv_m, recv_s = packed[..., :fates], packed[..., fates], packed[..., fates + 1]
        top = jnp.maximum(keep_m, recv_m)
        keep_f = jnp.exp(keep_m - top)
        recv_f = jnp.exp(recv_m - top)
        maxima = top
        totals = keep_s * keep_f + recv_s * recv_f
        weighted = keep_w * keep_f[..., None] + recv_w * recv_f[..., None]
    return maxima, totals, weighted


def body_split(sources, source_mass, targets, target_mass, fate_panel):
    src_count = sources.shape[0]
    tgt_count = targets.shape[0]
    all_sources = src_count * lax.axis_size("rows")
    all_targets = tgt_count * lax.axis_size(("cols", "rep"))
    log_a = jnp.log(source_mass / all_sources)
    log_b = jnp.log(target_mass / all_targets)
    src_sq = jnp.sum(sources * sources, axis=1)
    tgt_sq = jnp.sum(targets * targets, axis=1)
    cost = pair_cost(sources, src_sq, targets, tgt_sq)

    g_pot = jnp.zeros((tgt_count,), jnp.float32)
    f_pot = jnp.zeros((src_count,), jnp.float32)
    for iteration in range(ITERS):
        scores = log_b[None, :] + (g_pot[None, :] - cost) / entropic
        maxima = jnp.max(scores, axis=1)
        totals = jnp.sum(jnp.exp(scores - maxima[:, None]), axis=1)
        peak, whole = lse_allreduce(maxima, totals, ("rep", "cols"))
        f_pot = -relaxed * entropic * (peak + jnp.log(whole))

        scores = log_a[:, None] + (f_pot[:, None] - cost) / entropic
        maxima = jnp.max(scores, axis=0)
        totals = jnp.sum(jnp.exp(scores - maxima[None, :]), axis=0)
        peak, whole = lse_allreduce(maxima, totals, ("rows",))
        g_pot = -relaxed * entropic * (peak + jnp.log(whole))

    return (f_pot,) + fate_pullback(cost, log_b, g_pot, fate_panel)


def lse_scatter_exchange(maxima, totals, weighted, name):
    size = lax.axis_size(name)
    index = lax.axis_index(name)
    fates = weighted.shape[-1]
    packed = jnp.concatenate([weighted, maxima[..., None], totals[..., None]], axis=-1)
    parts = [lax.dynamic_index_in_dim(packed, index, axis=0, keepdims=False)]
    for shift in range(1, size):
        perm = [(i, (i + shift) % size) for i in range(size)]
        send = lax.dynamic_index_in_dim(packed, (index + shift) % size, axis=0, keepdims=False)
        parts.append(lax.ppermute(send, name, perm))
    top = parts[0][..., fates]
    for part in parts[1:]:
        top = jnp.maximum(top, part[..., fates])
    totals = None
    weighted = None
    for part in parts:
        factor = jnp.exp(part[..., fates] - top)
        add_s = part[..., fates + 1] * factor
        add_w = part[..., :fates] * factor[..., None]
        totals = add_s if totals is None else totals + add_s
        weighted = add_w if weighted is None else weighted + add_w
    return top, totals, weighted


def fate_pullback(cost, log_b, g_pot, fate_panel):
    src_count = cost.shape[0]
    scores = log_b[None, :] + (g_pot[None, :] - cost) / entropic
    maxima = jnp.max(scores, axis=1)
    weights = jnp.exp(scores - maxima[:, None])
    totals = jnp.sum(weights, axis=1)
    weighted = jnp.dot(
        weights, fate_panel, precision=lax.Precision.HIGHEST, preferred_element_type=jnp.float32
    )
    col_size = lax.axis_size("cols")
    rep_size = lax.axis_size("rep")
    fates = fate_panel.shape[1]
    if rep_size == 2 and col_size <= 8:
        block = src_count // (col_size * rep_size)
        maxima = jnp.swapaxes(maxima.reshape(col_size, rep_size, block), 0, 1)
        totals = jnp.swapaxes(totals.reshape(col_size, rep_size, block), 0, 1)
        weighted = jnp.swapaxes(weighted.reshape(col_size, rep_size, block, fates), 0, 1)
        maxima, totals, weighted = lse_halving(maxima, totals, weighted, [("rep", 1)])
        maxima, totals, weighted = lse_scatter_exchange(maxima, totals, weighted, "cols")
        fate_rows = weighted / totals[:, None]
    elif is_pow2(col_size) and is_pow2(rep_size):
        col_bits = col_size.bit_length() - 1
        rep_bits = rep_size.bit_length() - 1
        lead = (2,) * (col_bits + rep_bits)
        block = src_count // (col_size * rep_size)
        maxima = maxima.reshape(lead + (block,))
        totals = totals.reshape(lead + (block,))
        weighted = weighted.reshape(lead + (block, fates))
        order = [("cols", 1 << b) for b in range(col_bits - 1, -1, -1)]
        order += [("rep", 1 << b) for b in range(rep_bits - 1, -1, -1)]
        plan = list(range(len(order) - 1, col_bits - 1, -1)) + list(range(col_bits - 1, -1, -1))
        perm_dims = plan + list(range(len(order), len(order) + 1))
        maxima = jnp.transpose(maxima, perm_dims)
        totals = jnp.transpose(totals, perm_dims)
        weighted = jnp.transpose(weighted, perm_dims + [len(order) + 1])
        maxima, totals, weighted = lse_halving(
            maxima, totals, weighted, [order[d] for d in plan]
        )
        fate_rows = weighted / totals[:, None]
    else:
        whole_peak = lax.pmax(maxima, ("cols", "rep"))
        factor = jnp.exp(maxima - whole_peak)
        part_weighted, part_total = (
            lax.psum_scatter(
                weighted * factor[:, None], ("cols", "rep"), scatter_dimension=0, tiled=True
            ),
            lax.psum_scatter(totals * factor, ("cols", "rep"), scatter_dimension=0, tiled=True),
        )
        fate_rows = part_weighted / part_total[:, None]
    return (g_pot, fate_rows)


ROW_AXES = (("rep",), ("cols",))


def body(sources, source_mass, targets, target_mass, fate_panel):
    row_count = lax.axis_size("rows")
    if row_count != 2 or lax.axis_size("cols") > 8:
        return body_split(sources, source_mass, targets, target_mass, fate_panel)
    src_count = sources.shape[0]
    tgt_count = targets.shape[0]
    row = lax.axis_index("rows")
    mine = jnp.concatenate([sources, source_mass[:, None]], axis=1)
    theirs = lax.ppermute(mine, "rows", [(0, 1), (1, 0)])
    first = jnp.where(row == 0, mine, theirs)
    second = jnp.where(row == 0, theirs, mine)
    gathered = jnp.concatenate([first, second], axis=0)
    all_src = gathered[:, : sources.shape[1]]
    all_mass = gathered[:, sources.shape[1]]
    all_sources = src_count * row_count
    all_targets = tgt_count * lax.axis_size(("cols", "rep"))
    log_a = jnp.log(all_mass / all_sources)
    log_b = jnp.log(target_mass / all_targets)
    src_sq = jnp.sum(all_src * all_src, axis=1)
    tgt_sq = jnp.sum(targets * targets, axis=1)
    cost = pair_cost(all_src, src_sq, targets, tgt_sq)

    g_pot = jnp.zeros((tgt_count,), jnp.float32)
    f_all = jnp.zeros((all_sources,), jnp.float32)
    for iteration in range(ITERS):
        scores = log_b[None, :] + (g_pot[None, :] - cost) / entropic
        maxima = jnp.max(scores, axis=1)
        totals = jnp.sum(jnp.exp(scores - maxima[:, None]), axis=1)
        for axes in ROW_AXES:
            if len(axes) == 1 and lax.axis_size(axes[0]) == 2:
                maxima, totals = lse_allreduce(maxima, totals, axes)
            else:
                maxima, totals = lse_exchange(maxima, totals, axes)
        f_all = -relaxed * entropic * (maxima + jnp.log(totals))

        scores = log_a[:, None] + (f_all[:, None] - cost) / entropic
        maxima = jnp.max(scores, axis=0)
        totals = jnp.sum(jnp.exp(scores - maxima[None, :]), axis=0)
        g_pot = -relaxed * entropic * (maxima + jnp.log(totals))

    f_pot = lax.dynamic_slice_in_dim(f_all, row * src_count, src_count)
    cost_mine = lax.dynamic_slice_in_dim(cost, row * src_count, src_count, axis=0)
    return (f_pot,) + fate_pullback(cost_mine, log_b, g_pot, fate_panel)


def solution(mesh):
    in_specs = (
        P(("parts", "rows"), None),
        P(("parts", "rows")),
        P(("parts", "cols", "rep"), None),
        P(("parts", "cols", "rep")),
        P(("parts", "cols", "rep"), None),
    )
    out_specs = (
        P(("parts", "rows")),
        P(("parts", "cols", "rep")),
        P(("parts", "rows", "cols", "rep"), None),
    )
    return jax.shard_map(body, mesh=mesh, in_specs=in_specs, out_specs=out_specs, check_vma=False)
```

```python
import jax
import jax.numpy as jnp
from jax import lax
from jax.sharding import PartitionSpec as P

ITERS = 8


entropic = 0.1
relaxed = 1.0 / 1.1


def pair_cost(lhs_rows, lhs_sq, rhs_rows, rhs_sq):
    products = lax.dot_general(
        lhs_rows,
        rhs_rows,
        (((1,), (1,)), ((), ())),
        precision=lax.Precision.HIGHEST,
        preferred_element_type=jnp.float32,
    )
    return (lhs_sq[:, None] + rhs_sq[None, :] - 2.0 * products) / lhs_rows.shape[1]


def is_pow2(n):
    return n > 0 and (n & (n - 1)) == 0


def merge(m_one, s_one, m_two, s_two):
    top = jnp.maximum(m_one, m_two)
    return top, s_one * jnp.exp(m_one - top) + s_two * jnp.exp(m_two - top)


def lse_allreduce(maxima, totals, axes):
    if not all(is_pow2(lax.axis_size(name)) for name in axes):
        peak = lax.pmax(maxima, axes)
        return peak, lax.psum(totals * jnp.exp(maxima - peak), axes)
    for name in axes:
        size = lax.axis_size(name)
        index = lax.axis_index(name)
        step = 1
        while step < size:
            perm = [(i, i ^ step) for i in range(size)]
            other = lax.ppermute(jnp.stack([maxima, totals]), name, perm)
            other_m, other_s = other[0], other[1]
            low = (index & step) == 0
            lo_m = jnp.where(low, maxima, other_m)
            hi_m = jnp.where(low, other_m, maxima)
            lo_s = jnp.where(low, totals, other_s)
            hi_s = jnp.where(low, other_s, totals)
            maxima, totals = merge(lo_m, lo_s, hi_m, hi_s)
            step *= 2
    return maxima, totals


def lse_exchange(maxima, totals, axes):
    size = lax.axis_size(axes)
    index = lax.axis_index(axes)
    payload = jnp.stack([maxima, totals])
    received = [payload]
    for shift in range(1, size):
        perm = [(i, (i + shift) % size) for i in range(size)]
        received.append(lax.ppermute(payload, axes, perm))
    received = jnp.stack(received)
    ordered = [
        lax.dynamic_index_in_dim(received, (index - rank) % size, axis=0, keepdims=False)
        for rank in range(size)
    ]
    peak = ordered[0][0]
    for item in ordered[1:]:
        peak = jnp.maximum(peak, item[0])
    whole = ordered[0][1] * jnp.exp(ordered[0][0] - peak)
    for item in ordered[1:]:
        whole = whole + item[1] * jnp.exp(item[0] - peak)
    return peak, whole


def lse_halving(maxima, totals, weighted, dims):
    for name, step in dims:
        size = lax.axis_size(name)
        perm = [(i, i ^ step) for i in range(size)]
        high = (lax.axis_index(name) & step) != 0

        def split(x):
            lower = lax.index_in_dim(x, 0, axis=0, keepdims=False)
            upper = lax.index_in_dim(x, 1, axis=0, keepdims=False)
            return jnp.where(high, upper, lower), jnp.where(high, lower, upper)

        keep_m, send_m = split(maxima)
        keep_s, send_s = split(totals)
        keep_w, send_w = split(weighted)
        packed = jnp.concatenate([send_w, send_m[..., None], send_s[..., None]], axis=-1)
        packed = lax.ppermute(packed, name, perm)
        fates = weighted.shape[-1]
        recv_w, recv_m, recv_s = packed[..., :fates], packed[..., fates], packed[..., fates + 1]
        top = jnp.maximum(keep_m, recv_m)
        keep_f = jnp.exp(keep_m - top)
        recv_f = jnp.exp(recv_m - top)
        maxima = top
        totals = keep_s * keep_f + recv_s * recv_f
        weighted = keep_w * keep_f[..., None] + recv_w * recv_f[..., None]
    return maxima, totals, weighted


def body_split(sources, source_mass, targets, target_mass, fate_panel):
    src_count = sources.shape[0]
    tgt_count = targets.shape[0]
    all_sources = src_count * lax.axis_size("rows")
    all_targets = tgt_count * lax.axis_size(("cols", "rep"))
    log_a = jnp.log(source_mass / all_sources)
    log_b = jnp.log(target_mass / all_targets)
    src_sq = jnp.sum(sources * sources, axis=1)
    tgt_sq = jnp.sum(targets * targets, axis=1)
    cost = pair_cost(sources, src_sq, targets, tgt_sq)

    g_pot = jnp.zeros((tgt_count,), jnp.float32)
    f_pot = jnp.zeros((src_count,), jnp.float32)
    for _ in range(ITERS):
        scores = log_b[None, :] + (g_pot[None, :] - cost) / entropic
        maxima = jnp.max(scores, axis=1)
        totals = jnp.sum(jnp.exp(scores - maxima[:, None]), axis=1)
        peak, whole = lse_allreduce(maxima, totals, ("rep", "cols"))
        f_pot = -relaxed * entropic * (peak + jnp.log(whole))

        scores = log_a[:, None] + (f_pot[:, None] - cost) / entropic
        maxima = jnp.max(scores, axis=0)
        totals = jnp.sum(jnp.exp(scores - maxima[None, :]), axis=0)
        peak, whole = lse_allreduce(maxima, totals, ("rows",))
        g_pot = -relaxed * entropic * (peak + jnp.log(whole))

    return (f_pot,) + fate_pullback(cost, log_b, g_pot, fate_panel)


def lse_scatter_exchange(maxima, totals, weighted, name):
    size = lax.axis_size(name)
    index = lax.axis_index(name)
    fates = weighted.shape[-1]
    packed = jnp.concatenate([weighted, maxima[..., None], totals[..., None]], axis=-1)
    parts = [lax.dynamic_index_in_dim(packed, index, axis=0, keepdims=False)]
    for shift in range(1, size):
        perm = [(i, (i + shift) % size) for i in range(size)]
        send = lax.dynamic_index_in_dim(packed, (index + shift) % size, axis=0, keepdims=False)
        parts.append(lax.ppermute(send, name, perm))
    top = parts[0][..., fates]
    for part in parts[1:]:
        top = jnp.maximum(top, part[..., fates])
    totals = None
    weighted = None
    for part in parts:
        factor = jnp.exp(part[..., fates] - top)
        add_s = part[..., fates + 1] * factor
        add_w = part[..., :fates] * factor[..., None]
        totals = add_s if totals is None else totals + add_s
        weighted = add_w if weighted is None else weighted + add_w
    return top, totals, weighted


def fate_pullback(cost, log_b, g_pot, fate_panel):
    src_count = cost.shape[0]
    scores = log_b[None, :] + (g_pot[None, :] - cost) / entropic
    maxima = jnp.max(scores, axis=1)
    weights = jnp.exp(scores - maxima[:, None])
    totals = jnp.sum(weights, axis=1)
    weighted = jnp.dot(
        weights, fate_panel, precision=lax.Precision.HIGHEST, preferred_element_type=jnp.float32
    )
    col_size = lax.axis_size("cols")
    rep_size = lax.axis_size("rep")
    fates = fate_panel.shape[1]
    if rep_size == 2 and col_size <= 8:
        block = src_count // (col_size * rep_size)
        maxima = jnp.swapaxes(maxima.reshape(col_size, rep_size, block), 0, 1)
        totals = jnp.swapaxes(totals.reshape(col_size, rep_size, block), 0, 1)
        weighted = jnp.swapaxes(weighted.reshape(col_size, rep_size, block, fates), 0, 1)
        maxima, totals, weighted = lse_halving(maxima, totals, weighted, [("rep", 1)])
        maxima, totals, weighted = lse_scatter_exchange(maxima, totals, weighted, "cols")
        fate_rows = weighted / totals[:, None]
    elif is_pow2(col_size) and is_pow2(rep_size):
        col_bits = col_size.bit_length() - 1
        rep_bits = rep_size.bit_length() - 1
        lead = (2,) * (col_bits + rep_bits)
        block = src_count // (col_size * rep_size)
        maxima = maxima.reshape(lead + (block,))
        totals = totals.reshape(lead + (block,))
        weighted = weighted.reshape(lead + (block, fates))
        order = [("cols", 1 << b) for b in range(col_bits - 1, -1, -1)]
        order += [("rep", 1 << b) for b in range(rep_bits - 1, -1, -1)]
        plan = list(range(len(order) - 1, col_bits - 1, -1)) + list(range(col_bits - 1, -1, -1))
        perm_dims = plan + list(range(len(order), len(order) + 1))
        maxima = jnp.transpose(maxima, perm_dims)
        totals = jnp.transpose(totals, perm_dims)
        weighted = jnp.transpose(weighted, perm_dims + [len(order) + 1])
        maxima, totals, weighted = lse_halving(
            maxima, totals, weighted, [order[d] for d in plan]
        )
        fate_rows = weighted / totals[:, None]
    else:
        whole_peak = lax.pmax(maxima, ("cols", "rep"))
        factor = jnp.exp(maxima - whole_peak)
        part_weighted, part_total = (
            lax.psum_scatter(
                weighted * factor[:, None], ("cols", "rep"), scatter_dimension=0, tiled=True
            ),
            lax.psum_scatter(totals * factor, ("cols", "rep"), scatter_dimension=0, tiled=True),
        )
        fate_rows = part_weighted / part_total[:, None]
    return (g_pot, fate_rows)


ROW_AXES = (("rep",), ("cols",))


def row_reduce(maxima, totals):
    for axes in ROW_AXES:
        if len(axes) == 1 and lax.axis_size(axes[0]) == 2:
            maxima, totals = lse_allreduce(maxima, totals, axes)
        else:
            maxima, totals = lse_exchange(maxima, totals, axes)
    return maxima, totals


def body(sources, source_mass, targets, target_mass, fate_panel):
    row_count = lax.axis_size("rows")
    if row_count != 2 or lax.axis_size("cols") > 8:
        return body_split(sources, source_mass, targets, target_mass, fate_panel)
    src_count = sources.shape[0]
    tgt_count = targets.shape[0]
    row = lax.axis_index("rows")
    swap = [(0, 1), (1, 0)]
    mine = jnp.concatenate([sources, source_mass[:, None]], axis=1)
    theirs = lax.ppermute(mine, "rows", swap)
    all_sources = src_count * row_count
    all_targets = tgt_count * lax.axis_size(("cols", "rep"))
    log_b = jnp.log(target_mass / all_targets)
    tgt_sq = jnp.sum(targets * targets, axis=1)
    g_pot = jnp.zeros((tgt_count,), jnp.float32)

    own_sq = jnp.sum(sources * sources, axis=1)
    own_cost = pair_cost(sources, own_sq, targets, tgt_sq)
    scores = log_b[None, :] + (g_pot[None, :] - own_cost) / entropic
    maxima = jnp.max(scores, axis=1)
    totals = jnp.sum(jnp.exp(scores - maxima[:, None]), axis=1)
    maxima, totals = row_reduce(maxima, totals)
    f_own = -relaxed * entropic * (maxima + jnp.log(totals))
    f_theirs = lax.ppermute(f_own, "rows", swap)
    f_all = jnp.concatenate(
        [jnp.where(row == 0, f_own, f_theirs), jnp.where(row == 0, f_theirs, f_own)]
    )

    first = jnp.where(row == 0, mine, theirs)
    second = jnp.where(row == 0, theirs, mine)
    gathered = jnp.concatenate([first, second], axis=0)
    all_src = gathered[:, : sources.shape[1]]
    all_mass = gathered[:, sources.shape[1]]
    log_a = jnp.log(all_mass / all_sources)
    src_sq = jnp.sum(all_src * all_src, axis=1)
    cost = pair_cost(all_src, src_sq, targets, tgt_sq)

    for iteration in range(ITERS):
        if iteration > 0:
            scores = log_b[None, :] + (g_pot[None, :] - cost) / entropic
            maxima = jnp.max(scores, axis=1)
            totals = jnp.sum(jnp.exp(scores - maxima[:, None]), axis=1)
            maxima, totals = row_reduce(maxima, totals)
            f_all = -relaxed * entropic * (maxima + jnp.log(totals))

        scores = log_a[:, None] + (f_all[:, None] - cost) / entropic
        maxima = jnp.max(scores, axis=0)
        totals = jnp.sum(jnp.exp(scores - maxima[None, :]), axis=0)
        g_pot = -relaxed * entropic * (maxima + jnp.log(totals))

    f_pot = lax.dynamic_slice_in_dim(f_all, row * src_count, src_count)
    return (f_pot,) + fate_pullback(own_cost, log_b, g_pot, fate_panel)


def solution(mesh):
    in_specs = (
        P(("parts", "rows"), None),
        P(("parts", "rows")),
        P(("parts", "cols", "rep"), None),
        P(("parts", "cols", "rep")),
        P(("parts", "cols", "rep"), None),
    )
    out_specs = (
        P(("parts", "rows")),
        P(("parts", "cols", "rep")),
        P(("parts", "rows", "cols", "rep"), None),
    )

    return jax.shard_map(body, mesh=mesh, in_specs=in_specs, out_specs=out_specs, check_vma=False)
```

```python
import jax
import jax.numpy as jnp
from jax import lax
from jax.sharding import PartitionSpec as P

ITERS = 8


entropic = 0.1
relaxed = 1.0 / 1.1


def pair_cost(lhs_rows, lhs_sq, rhs_rows, rhs_sq):
    products = lax.dot_general(
        lhs_rows,
        rhs_rows,
        (((1,), (1,)), ((), ())),
        precision=lax.Precision.HIGHEST,
        preferred_element_type=jnp.float32,
    )
    return (lhs_sq[:, None] + rhs_sq[None, :] - 2.0 * products) / lhs_rows.shape[1]


def is_pow2(n):
    return n > 0 and (n & (n - 1)) == 0


def merge(m_one, s_one, m_two, s_two):
    top = jnp.maximum(m_one, m_two)
    return top, s_one * jnp.exp(m_one - top) + s_two * jnp.exp(m_two - top)


def lse_allreduce(maxima, totals, axes):
    if not all(is_pow2(lax.axis_size(name)) for name in axes):
        peak = lax.pmax(maxima, axes)
        return peak, lax.psum(totals * jnp.exp(maxima - peak), axes)
    for name in axes:
        size = lax.axis_size(name)
        index = lax.axis_index(name)
        step = 1
        while step < size:
            perm = [(i, i ^ step) for i in range(size)]
            other = lax.ppermute(jnp.stack([maxima, totals]), name, perm)
            other_m, other_s = other[0], other[1]
            low = (index & step) == 0
            lo_m = jnp.where(low, maxima, other_m)
            hi_m = jnp.where(low, other_m, maxima)
            lo_s = jnp.where(low, totals, other_s)
            hi_s = jnp.where(low, other_s, totals)
            maxima, totals = merge(lo_m, lo_s, hi_m, hi_s)
            step *= 2
    return maxima, totals


def lse_exchange(maxima, totals, axes):
    size = lax.axis_size(axes)
    index = lax.axis_index(axes)
    payload = jnp.stack([maxima, totals])
    received = [payload]
    for shift in range(1, size):
        perm = [(i, (i + shift) % size) for i in range(size)]
        received.append(lax.ppermute(payload, axes, perm))
    received = jnp.stack(received)
    ordered = [
        lax.dynamic_index_in_dim(received, (index - rank) % size, axis=0, keepdims=False)
        for rank in range(size)
    ]
    peak = ordered[0][0]
    for item in ordered[1:]:
        peak = jnp.maximum(peak, item[0])
    whole = ordered[0][1] * jnp.exp(ordered[0][0] - peak)
    for item in ordered[1:]:
        whole = whole + item[1] * jnp.exp(item[0] - peak)
    return peak, whole


def lse_halving(maxima, totals, weighted, dims):
    for name, step in dims:
        size = lax.axis_size(name)
        perm = [(i, i ^ step) for i in range(size)]
        high = (lax.axis_index(name) & step) != 0

        def split(x):
            lower = lax.index_in_dim(x, 0, axis=0, keepdims=False)
            upper = lax.index_in_dim(x, 1, axis=0, keepdims=False)
            return jnp.where(high, upper, lower), jnp.where(high, lower, upper)

        keep_m, send_m = split(maxima)
        keep_s, send_s = split(totals)
        keep_w, send_w = split(weighted)
        packed = jnp.concatenate([send_w, send_m[..., None], send_s[..., None]], axis=-1)
        packed = lax.ppermute(packed, name, perm)
        fates = weighted.shape[-1]
        recv_w, recv_m, recv_s = packed[..., :fates], packed[..., fates], packed[..., fates + 1]
        top = jnp.maximum(keep_m, recv_m)
        keep_f = jnp.exp(keep_m - top)
        recv_f = jnp.exp(recv_m - top)
        maxima = top
        totals = keep_s * keep_f + recv_s * recv_f
        weighted = keep_w * keep_f[..., None] + recv_w * recv_f[..., None]
    return maxima, totals, weighted


def body_split(sources, source_mass, targets, target_mass, fate_panel):
    src_count = sources.shape[0]
    tgt_count = targets.shape[0]
    all_sources = src_count * lax.axis_size("rows")
    all_targets = tgt_count * lax.axis_size(("cols", "rep"))
    log_a = jnp.log(source_mass / all_sources)
    log_b = jnp.log(target_mass / all_targets)
    src_sq = jnp.sum(sources * sources, axis=1)
    tgt_sq = jnp.sum(targets * targets, axis=1)
    cost = pair_cost(sources, src_sq, targets, tgt_sq)

    g_pot = jnp.zeros((tgt_count,), jnp.float32)
    f_pot = jnp.zeros((src_count,), jnp.float32)
    for iteration in range(ITERS):
        scores = log_b[None, :] + (g_pot[None, :] - cost) / entropic
        maxima = jnp.max(scores, axis=1)
        totals = jnp.sum(jnp.exp(scores - maxima[:, None]), axis=1)
        peak, whole = lse_allreduce(maxima, totals, ("rep", "cols"))
        f_pot = -relaxed * entropic * (peak + jnp.log(whole))

        scores = log_a[:, None] + (f_pot[:, None] - cost) / entropic
        maxima = jnp.max(scores, axis=0)
        totals = jnp.sum(jnp.exp(scores - maxima[None, :]), axis=0)
        peak, whole = lse_allreduce(maxima, totals, ("rows",))
        g_pot = -relaxed * entropic * (peak + jnp.log(whole))

    return (f_pot,) + fate_pullback(cost, log_b, g_pot, fate_panel)


def lse_scatter_exchange(maxima, totals, weighted, name):
    size = lax.axis_size(name)
    index = lax.axis_index(name)
    fates = weighted.shape[-1]
    packed = jnp.concatenate([weighted, maxima[..., None], totals[..., None]], axis=-1)
    parts = [lax.dynamic_index_in_dim(packed, index, axis=0, keepdims=False)]
    for shift in range(1, size):
        perm = [(i, (i + shift) % size) for i in range(size)]
        send = lax.dynamic_index_in_dim(packed, (index + shift) % size, axis=0, keepdims=False)
        parts.append(lax.ppermute(send, name, perm))
    top = parts[0][..., fates]
    for part in parts[1:]:
        top = jnp.maximum(top, part[..., fates])
    totals = None
    weighted = None
    for part in parts:
        factor = jnp.exp(part[..., fates] - top)
        add_s = part[..., fates + 1] * factor
        add_w = part[..., :fates] * factor[..., None]
        totals = add_s if totals is None else totals + add_s
        weighted = add_w if weighted is None else weighted + add_w
    return top, totals, weighted


def fate_pullback(cost, log_b, g_pot, fate_panel, scaled=False):
    src_count = cost.shape[0]
    if scaled:
        scores = (log_b + g_pot / entropic)[None, :] - cost
    else:
        scores = log_b[None, :] + (g_pot[None, :] - cost) / entropic
    maxima = jnp.max(scores, axis=1)
    weights = jnp.exp(scores - maxima[:, None])
    totals = jnp.sum(weights, axis=1)
    weighted = jnp.dot(
        weights, fate_panel, precision=lax.Precision.HIGHEST, preferred_element_type=jnp.float32
    )
    col_size = lax.axis_size("cols")
    rep_size = lax.axis_size("rep")
    fates = fate_panel.shape[1]
    if rep_size == 2 and col_size <= 8:
        block = src_count // (col_size * rep_size)
        maxima = jnp.swapaxes(maxima.reshape(col_size, rep_size, block), 0, 1)
        totals = jnp.swapaxes(totals.reshape(col_size, rep_size, block), 0, 1)
        weighted = jnp.swapaxes(weighted.reshape(col_size, rep_size, block, fates), 0, 1)
        maxima, totals, weighted = lse_halving(maxima, totals, weighted, [("rep", 1)])
        maxima, totals, weighted = lse_scatter_exchange(maxima, totals, weighted, "cols")
        fate_rows = weighted / totals[:, None]
    elif is_pow2(col_size) and is_pow2(rep_size):
        col_bits = col_size.bit_length() - 1
        rep_bits = rep_size.bit_length() - 1
        lead = (2,) * (col_bits + rep_bits)
        block = src_count // (col_size * rep_size)
        maxima = maxima.reshape(lead + (block,))
        totals = totals.reshape(lead + (block,))
        weighted = weighted.reshape(lead + (block, fates))
        order = [("cols", 1 << b) for b in range(col_bits - 1, -1, -1)]
        order += [("rep", 1 << b) for b in range(rep_bits - 1, -1, -1)]
        plan = list(range(len(order) - 1, col_bits - 1, -1)) + list(range(col_bits - 1, -1, -1))
        perm_dims = plan + list(range(len(order), len(order) + 1))
        maxima = jnp.transpose(maxima, perm_dims)
        totals = jnp.transpose(totals, perm_dims)
        weighted = jnp.transpose(weighted, perm_dims + [len(order) + 1])
        maxima, totals, weighted = lse_halving(
            maxima, totals, weighted, [order[d] for d in plan]
        )
        fate_rows = weighted / totals[:, None]
    else:
        whole_peak = lax.pmax(maxima, ("cols", "rep"))
        factor = jnp.exp(maxima - whole_peak)
        part_weighted, part_total = (
            lax.psum_scatter(
                weighted * factor[:, None], ("cols", "rep"), scatter_dimension=0, tiled=True
            ),
            lax.psum_scatter(totals * factor, ("cols", "rep"), scatter_dimension=0, tiled=True),
        )
        fate_rows = part_weighted / part_total[:, None]
    return (g_pot, fate_rows)


ROW_AXES = (("rep",), ("cols",))


def row_reduce(maxima, totals):
    for axes in ROW_AXES:
        if len(axes) == 1 and lax.axis_size(axes[0]) == 2:
            maxima, totals = lse_allreduce(maxima, totals, axes)
        else:
            maxima, totals = lse_exchange(maxima, totals, axes)
    return maxima, totals


def body(sources, source_mass, targets, target_mass, fate_panel):
    row_count = lax.axis_size("rows")
    if row_count != 2 or lax.axis_size("cols") > 8:
        return body_split(sources, source_mass, targets, target_mass, fate_panel)
    src_count = sources.shape[0]
    tgt_count = targets.shape[0]
    row = lax.axis_index("rows")
    mine = jnp.concatenate([sources, source_mass[:, None]], axis=1)
    theirs = lax.ppermute(mine, "rows", [(0, 1), (1, 0)])
    first = jnp.where(row == 0, mine, theirs)
    second = jnp.where(row == 0, theirs, mine)
    gathered = jnp.concatenate([first, second], axis=0)
    all_src = gathered[:, : sources.shape[1]]
    all_mass = gathered[:, sources.shape[1]]
    all_sources = src_count * row_count
    all_targets = tgt_count * lax.axis_size(("cols", "rep"))
    log_a = jnp.log(all_mass / all_sources)
    log_b = jnp.log(target_mass / all_targets)
    src_sq = jnp.sum(all_src * all_src, axis=1)
    tgt_sq = jnp.sum(targets * targets, axis=1)
    cost = pair_cost(all_src, src_sq, targets, tgt_sq)

    scaled = cost / entropic
    g_pot = jnp.zeros((tgt_count,), jnp.float32)
    f_all = jnp.zeros((all_sources,), jnp.float32)
    for iteration in range(ITERS):
        scores = (log_b + g_pot / entropic)[None, :] - scaled
        maxima = jnp.max(scores, axis=1)
        totals = jnp.sum(jnp.exp(scores - maxima[:, None]), axis=1)
        maxima, totals = row_reduce(maxima, totals)
        f_all = -relaxed * entropic * (maxima + jnp.log(totals))

        scores = (log_a + f_all / entropic)[:, None] - scaled
        maxima = jnp.max(scores, axis=0)
        totals = jnp.sum(jnp.exp(scores - maxima[None, :]), axis=0)
        g_pot = -relaxed * entropic * (maxima + jnp.log(totals))

    f_pot = lax.dynamic_slice_in_dim(f_all, row * src_count, src_count)
    scaled_mine = lax.dynamic_slice_in_dim(scaled, row * src_count, src_count, axis=0)
    return (f_pot,) + fate_pullback(scaled_mine, log_b, g_pot, fate_panel, scaled=True)


def solution(mesh):
    in_specs = (
        P(("parts", "rows"), None),
        P(("parts", "rows")),
        P(("parts", "cols", "rep"), None),
        P(("parts", "cols", "rep")),
        P(("parts", "cols", "rep"), None),
    )
    out_specs = (
        P(("parts", "rows")),
        P(("parts", "cols", "rep")),
        P(("parts", "rows", "cols", "rep"), None),
    )
    return jax.shard_map(body, mesh=mesh, in_specs=in_specs, out_specs=out_specs, check_vma=False)
```

```python
import jax
import jax.numpy as jnp
from jax import lax
from jax.experimental.layout import Layout, with_layout_constraint
from jax.sharding import PartitionSpec as P

ITERS = 8


entropic = 0.1
relaxed = 1.0 / 1.1


def pair_cost(lhs_rows, lhs_sq, rhs_rows, rhs_sq):
    products = lax.dot_general(
        lhs_rows,
        rhs_rows,
        (((1,), (1,)), ((), ())),
        precision=lax.Precision.HIGHEST,
        preferred_element_type=jnp.float32,
    )
    return (lhs_sq[:, None] + rhs_sq[None, :] - 2.0 * products) / lhs_rows.shape[1]


def is_pow2(n):
    return n > 0 and (n & (n - 1)) == 0


def merge(m_one, s_one, m_two, s_two):
    top = jnp.maximum(m_one, m_two)
    return top, s_one * jnp.exp(m_one - top) + s_two * jnp.exp(m_two - top)


def lse_allreduce(maxima, totals, axes):
    if not all(is_pow2(lax.axis_size(name)) for name in axes):
        peak = lax.pmax(maxima, axes)
        return peak, lax.psum(totals * jnp.exp(maxima - peak), axes)
    for name in axes:
        size = lax.axis_size(name)
        index = lax.axis_index(name)
        step = 1
        while step < size:
            perm = [(i, i ^ step) for i in range(size)]
            other = lax.ppermute(jnp.stack([maxima, totals]), name, perm)
            other_m, other_s = other[0], other[1]
            low = (index & step) == 0
            lo_m = jnp.where(low, maxima, other_m)
            hi_m = jnp.where(low, other_m, maxima)
            lo_s = jnp.where(low, totals, other_s)
            hi_s = jnp.where(low, other_s, totals)
            maxima, totals = merge(lo_m, lo_s, hi_m, hi_s)
            step *= 2
    return maxima, totals


def lse_exchange(maxima, totals, axes):
    size = lax.axis_size(axes)
    index = lax.axis_index(axes)
    payload = jnp.stack([maxima, totals])
    received = [payload]
    for shift in range(1, size):
        perm = [(i, (i + shift) % size) for i in range(size)]
        received.append(lax.ppermute(payload, axes, perm))
    received = jnp.stack(received)
    ordered = [
        lax.dynamic_index_in_dim(received, (index - rank) % size, axis=0, keepdims=False)
        for rank in range(size)
    ]
    peak = ordered[0][0]
    for item in ordered[1:]:
        peak = jnp.maximum(peak, item[0])
    whole = ordered[0][1] * jnp.exp(ordered[0][0] - peak)
    for item in ordered[1:]:
        whole = whole + item[1] * jnp.exp(item[0] - peak)
    return peak, whole


def lse_halving(maxima, totals, weighted, dims):
    for name, step in dims:
        size = lax.axis_size(name)
        perm = [(i, i ^ step) for i in range(size)]
        high = (lax.axis_index(name) & step) != 0

        def split(x):
            lower = lax.index_in_dim(x, 0, axis=0, keepdims=False)
            upper = lax.index_in_dim(x, 1, axis=0, keepdims=False)
            return jnp.where(high, upper, lower), jnp.where(high, lower, upper)

        keep_m, send_m = split(maxima)
        keep_s, send_s = split(totals)
        keep_w, send_w = split(weighted)
        packed = jnp.concatenate([send_w, send_m[..., None], send_s[..., None]], axis=-1)
        packed = lax.ppermute(packed, name, perm)
        fates = weighted.shape[-1]
        recv_w, recv_m, recv_s = packed[..., :fates], packed[..., fates], packed[..., fates + 1]
        top = jnp.maximum(keep_m, recv_m)
        keep_f = jnp.exp(keep_m - top)
        recv_f = jnp.exp(recv_m - top)
        maxima = top
        totals = keep_s * keep_f + recv_s * recv_f
        weighted = keep_w * keep_f[..., None] + recv_w * recv_f[..., None]
    return maxima, totals, weighted


def body_split(sources, source_mass, targets, target_mass, fate_panel):
    src_count = sources.shape[0]
    tgt_count = targets.shape[0]
    all_sources = src_count * lax.axis_size("rows")
    all_targets = tgt_count * lax.axis_size(("cols", "rep"))
    log_a = jnp.log(source_mass / all_sources)
    log_b = jnp.log(target_mass / all_targets)
    src_sq = jnp.sum(sources * sources, axis=1)
    tgt_sq = jnp.sum(targets * targets, axis=1)
    cost = pair_cost(sources, src_sq, targets, tgt_sq)

    g_pot = jnp.zeros((tgt_count,), jnp.float32)
    f_pot = jnp.zeros((src_count,), jnp.float32)
    for _ in range(ITERS):
        scores = log_b[None, :] + (g_pot[None, :] - cost) / entropic
        maxima = jnp.max(scores, axis=1)
        totals = jnp.sum(jnp.exp(scores - maxima[:, None]), axis=1)
        peak, whole = lse_allreduce(maxima, totals, ("rep", "cols"))
        f_pot = -relaxed * entropic * (peak + jnp.log(whole))

        scores = log_a[:, None] + (f_pot[:, None] - cost) / entropic
        maxima = jnp.max(scores, axis=0)
        totals = jnp.sum(jnp.exp(scores - maxima[None, :]), axis=0)
        peak, whole = lse_allreduce(maxima, totals, ("rows",))
        g_pot = -relaxed * entropic * (peak + jnp.log(whole))

    return (f_pot,) + fate_pullback(cost, log_b, g_pot, fate_panel)


def lse_scatter_exchange(maxima, totals, weighted, name):
    size = lax.axis_size(name)
    index = lax.axis_index(name)
    fates = weighted.shape[-1]
    packed = jnp.concatenate([weighted, maxima[..., None], totals[..., None]], axis=-1)
    parts = [lax.dynamic_index_in_dim(packed, index, axis=0, keepdims=False)]
    for shift in range(1, size):
        perm = [(i, (i + shift) % size) for i in range(size)]
        send = lax.dynamic_index_in_dim(packed, (index + shift) % size, axis=0, keepdims=False)
        parts.append(lax.ppermute(send, name, perm))
    top = parts[0][..., fates]
    for part in parts[1:]:
        top = jnp.maximum(top, part[..., fates])
    totals = None
    weighted = None
    for part in parts:
        factor = jnp.exp(part[..., fates] - top)
        add_s = part[..., fates + 1] * factor
        add_w = part[..., :fates] * factor[..., None]
        totals = add_s if totals is None else totals + add_s
        weighted = add_w if weighted is None else weighted + add_w
    return top, totals, weighted


def fate_pullback(cost, log_b, g_pot, fate_panel, scaled=False):
    src_count = cost.shape[0]
    if scaled:
        scores = (log_b + g_pot / entropic)[None, :] - cost
    else:
        scores = log_b[None, :] + (g_pot[None, :] - cost) / entropic
    maxima = jnp.max(scores, axis=1)
    weights = jnp.exp(scores - maxima[:, None])
    totals = jnp.sum(weights, axis=1)
    weighted = jnp.dot(
        weights, fate_panel, precision=lax.Precision.HIGHEST, preferred_element_type=jnp.float32
    )
    col_size = lax.axis_size("cols")
    rep_size = lax.axis_size("rep")
    fates = fate_panel.shape[1]
    if rep_size == 2 and col_size <= 8:
        block = src_count // (col_size * rep_size)
        maxima = jnp.swapaxes(maxima.reshape(col_size, rep_size, block), 0, 1)
        totals = jnp.swapaxes(totals.reshape(col_size, rep_size, block), 0, 1)
        weighted = jnp.swapaxes(weighted.reshape(col_size, rep_size, block, fates), 0, 1)
        maxima, totals, weighted = lse_halving(maxima, totals, weighted, [("rep", 1)])
        maxima, totals, weighted = lse_scatter_exchange(maxima, totals, weighted, "cols")
        fate_rows = weighted / totals[:, None]
    elif is_pow2(col_size) and is_pow2(rep_size):
        col_bits = col_size.bit_length() - 1
        rep_bits = rep_size.bit_length() - 1
        lead = (2,) * (col_bits + rep_bits)
        block = src_count // (col_size * rep_size)
        maxima = maxima.reshape(lead + (block,))
        totals = totals.reshape(lead + (block,))
        weighted = weighted.reshape(lead + (block, fates))
        order = [("cols", 1 << b) for b in range(col_bits - 1, -1, -1)]
        order += [("rep", 1 << b) for b in range(rep_bits - 1, -1, -1)]
        plan = list(range(len(order) - 1, col_bits - 1, -1)) + list(range(col_bits - 1, -1, -1))
        perm_dims = plan + list(range(len(order), len(order) + 1))
        maxima = jnp.transpose(maxima, perm_dims)
        totals = jnp.transpose(totals, perm_dims)
        weighted = jnp.transpose(weighted, perm_dims + [len(order) + 1])
        maxima, totals, weighted = lse_halving(
            maxima, totals, weighted, [order[d] for d in plan]
        )
        fate_rows = weighted / totals[:, None]
    else:
        whole_peak = lax.pmax(maxima, ("cols", "rep"))
        factor = jnp.exp(maxima - whole_peak)
        part_weighted, part_total = (
            lax.psum_scatter(
                weighted * factor[:, None], ("cols", "rep"), scatter_dimension=0, tiled=True
            ),
            lax.psum_scatter(totals * factor, ("cols", "rep"), scatter_dimension=0, tiled=True),
        )
        fate_rows = part_weighted / part_total[:, None]
    return (g_pot, fate_rows)


ROW_AXES = (("rep",), ("cols",))


def row_reduce(maxima, totals):
    for axes in ROW_AXES:
        if len(axes) == 1 and lax.axis_size(axes[0]) == 2:
            maxima, totals = lse_allreduce(maxima, totals, axes)
        else:
            maxima, totals = lse_exchange(maxima, totals, axes)
    return maxima, totals


def body(sources, source_mass, targets, target_mass, fate_panel):
    row_count = lax.axis_size("rows")
    if row_count != 2 or lax.axis_size("cols") > 8:
        return body_split(sources, source_mass, targets, target_mass, fate_panel)
    src_count = sources.shape[0]
    tgt_count = targets.shape[0]
    row = lax.axis_index("rows")
    dim = sources.shape[1]
    mine = jnp.concatenate([sources, source_mass[:, None]], axis=1)
    theirs = lax.ppermute(mine, "rows", [(0, 1), (1, 0)])
    all_sources = src_count * row_count
    all_targets = tgt_count * lax.axis_size(("cols", "rep"))
    log_b = jnp.log(target_mass / all_targets)
    tgt_sq = jnp.sum(targets * targets, axis=1)

    def scaled_cost(src):
        src_sq = jnp.sum(src * src, axis=1)
        return pair_cost(src, src_sq, targets, tgt_sq) / entropic

    scaled_mine = scaled_cost(sources)
    log_a_mine = jnp.log(source_mass / all_sources)
    g_pot = jnp.zeros((tgt_count,), jnp.float32)
    scores = (log_b + g_pot / entropic)[None, :] - scaled_mine
    maxima = jnp.max(scores, axis=1)
    totals = jnp.sum(jnp.exp(scores - maxima[:, None]), axis=1)
    maxima, totals = row_reduce(maxima, totals)
    f_mine = -relaxed * entropic * (maxima + jnp.log(totals))
    scores = (log_a_mine + f_mine / entropic)[:, None] - scaled_mine
    maxima = jnp.max(scores, axis=0)
    totals = jnp.sum(jnp.exp(scores - maxima[None, :]), axis=0)
    maxima, totals = lse_allreduce(maxima, totals, ("rows",))
    g_pot = -relaxed * entropic * (maxima + jnp.log(totals))

    first = jnp.where(row == 0, mine, theirs)
    second = jnp.where(row == 0, theirs, mine)
    gathered = jnp.concatenate([first, second], axis=0)
    all_src = gathered[:, :dim]
    all_mass = gathered[:, dim]
    log_a = jnp.log(all_mass / all_sources)
    scaled = with_layout_constraint(scaled_cost(all_src), Layout(major_to_minor=(1, 0)))
    scaled, log_a = lax.optimization_barrier((scaled, log_a))

    for _ in range(1, ITERS):
        scores = (log_b + g_pot / entropic)[None, :] - scaled
        maxima = jnp.max(scores, axis=1)
        totals = jnp.sum(jnp.exp(scores - maxima[:, None]), axis=1)
        maxima, totals = row_reduce(maxima, totals)
        f_all = -relaxed * entropic * (maxima + jnp.log(totals))

        scores = (log_a + f_all / entropic)[:, None] - scaled
        maxima = jnp.max(scores, axis=0)
        totals = jnp.sum(jnp.exp(scores - maxima[None, :]), axis=0)
        g_pot = -relaxed * entropic * (maxima + jnp.log(totals))

    f_pot = lax.dynamic_slice_in_dim(f_all, row * src_count, src_count)
    return (f_pot,) + fate_pullback(scaled_mine, log_b, g_pot, fate_panel, scaled=True)


def solution(mesh):
    in_specs = (
        P(("parts", "rows"), None),
        P(("parts", "rows")),
        P(("parts", "cols", "rep"), None),
        P(("parts", "cols", "rep")),
        P(("parts", "cols", "rep"), None),
    )
    out_specs = (
        P(("parts", "rows")),
        P(("parts", "cols", "rep")),
        P(("parts", "rows", "cols", "rep"), None),
    )

    return jax.shard_map(body, mesh=mesh, in_specs=in_specs, out_specs=out_specs, check_vma=False)
```

```python
import jax
import jax.numpy as jnp
from jax import lax
from jax.experimental.layout import Layout, with_layout_constraint
from jax.sharding import PartitionSpec as P

ITERS = 8


entropic = 0.1
relaxed = 1.0 / 1.1


def pair_cost(lhs_rows, lhs_sq, rhs_rows, rhs_sq):
    products = lax.dot_general(
        lhs_rows,
        rhs_rows,
        (((1,), (1,)), ((), ())),
        precision=lax.Precision.HIGHEST,
        preferred_element_type=jnp.float32,
    )
    return (lhs_sq[:, None] + rhs_sq[None, :] - 2.0 * products) / lhs_rows.shape[1]


def is_pow2(n):
    return n > 0 and (n & (n - 1)) == 0


def merge(m_one, s_one, m_two, s_two):
    top = jnp.maximum(m_one, m_two)
    return top, s_one * jnp.exp(m_one - top) + s_two * jnp.exp(m_two - top)


def lse_allreduce(maxima, totals, axes):
    if not all(is_pow2(lax.axis_size(name)) for name in axes):
        peak = lax.pmax(maxima, axes)
        return peak, lax.psum(totals * jnp.exp(maxima - peak), axes)
    for name in axes:
        size = lax.axis_size(name)
        index = lax.axis_index(name)
        step = 1
        while step < size:
            perm = [(i, i ^ step) for i in range(size)]
            other = lax.ppermute(jnp.stack([maxima, totals]), name, perm)
            other_m, other_s = other[0], other[1]
            low = (index & step) == 0
            lo_m = jnp.where(low, maxima, other_m)
            hi_m = jnp.where(low, other_m, maxima)
            lo_s = jnp.where(low, totals, other_s)
            hi_s = jnp.where(low, other_s, totals)
            maxima, totals = merge(lo_m, lo_s, hi_m, hi_s)
            step *= 2
    return maxima, totals


def lse_exchange(maxima, totals, axes):
    size = lax.axis_size(axes)
    index = lax.axis_index(axes)
    payload = jnp.stack([maxima, totals])
    received = [payload]
    for mask in range(1, size):
        if is_pow2(size):
            perm = [(i, i ^ mask) for i in range(size)]
        else:
            perm = [(i, (i + mask) % size) for i in range(size)]
        received.append(lax.ppermute(payload, axes, perm))
    received = jnp.stack(received)
    if is_pow2(size):
        slots = [index ^ rank for rank in range(size)]
    else:
        slots = [(index - rank) % size for rank in range(size)]
    ordered = [lax.dynamic_index_in_dim(received, slot, axis=0, keepdims=False) for slot in slots]
    peak = ordered[0][0]
    for item in ordered[1:]:
        peak = jnp.maximum(peak, item[0])
    whole = ordered[0][1] * jnp.exp(ordered[0][0] - peak)
    for item in ordered[1:]:
        whole = whole + item[1] * jnp.exp(item[0] - peak)
    return peak, whole


def lse_halving(maxima, totals, weighted, dims):
    for name, step in dims:
        size = lax.axis_size(name)
        perm = [(i, i ^ step) for i in range(size)]
        high = (lax.axis_index(name) & step) != 0

        def split(x):
            lower = lax.index_in_dim(x, 0, axis=0, keepdims=False)
            upper = lax.index_in_dim(x, 1, axis=0, keepdims=False)
            return jnp.where(high, upper, lower), jnp.where(high, lower, upper)

        keep_m, send_m = split(maxima)
        keep_s, send_s = split(totals)
        keep_w, send_w = split(weighted)
        packed = jnp.concatenate([send_w, send_m[..., None], send_s[..., None]], axis=-1)
        packed = lax.ppermute(packed, name, perm)
        fates = weighted.shape[-1]
        recv_w, recv_m, recv_s = packed[..., :fates], packed[..., fates], packed[..., fates + 1]
        top = jnp.maximum(keep_m, recv_m)
        keep_f = jnp.exp(keep_m - top)
        recv_f = jnp.exp(recv_m - top)
        maxima = top
        totals = keep_s * keep_f + recv_s * recv_f
        weighted = keep_w * keep_f[..., None] + recv_w * recv_f[..., None]
    return maxima, totals, weighted


def body_split(sources, source_mass, targets, target_mass, fate_panel):
    src_count = sources.shape[0]
    tgt_count = targets.shape[0]
    all_sources = src_count * lax.axis_size("rows")
    all_targets = tgt_count * lax.axis_size(("cols", "rep"))
    log_a = jnp.log(source_mass / all_sources)
    log_b = jnp.log(target_mass / all_targets)
    src_sq = jnp.sum(sources * sources, axis=1)
    tgt_sq = jnp.sum(targets * targets, axis=1)
    cost = pair_cost(sources, src_sq, targets, tgt_sq)

    g_pot = jnp.zeros((tgt_count,), jnp.float32)
    f_pot = jnp.zeros((src_count,), jnp.float32)
    for _ in range(ITERS):
        scores = log_b[None, :] + (g_pot[None, :] - cost) / entropic
        maxima = jnp.max(scores, axis=1)
        totals = jnp.sum(jnp.exp(scores - maxima[:, None]), axis=1)
        peak, whole = lse_allreduce(maxima, totals, ("rep", "cols"))
        f_pot = -relaxed * entropic * (peak + jnp.log(whole))

        scores = log_a[:, None] + (f_pot[:, None] - cost) / entropic
        maxima = jnp.max(scores, axis=0)
        totals = jnp.sum(jnp.exp(scores - maxima[None, :]), axis=0)
        peak, whole = lse_allreduce(maxima, totals, ("rows",))
        g_pot = -relaxed * entropic * (peak + jnp.log(whole))

    return (f_pot,) + fate_pullback(cost, log_b, g_pot, fate_panel)


def lse_scatter_exchange(maxima, totals, weighted, name):
    size = lax.axis_size(name)
    index = lax.axis_index(name)
    fates = weighted.shape[-1]
    packed = jnp.concatenate([weighted, maxima[..., None], totals[..., None]], axis=-1)
    parts = [lax.dynamic_index_in_dim(packed, index, axis=0, keepdims=False)]
    for shift in range(1, size):
        if is_pow2(size):
            perm = [(i, i ^ shift) for i in range(size)]
            owner = index ^ shift
        else:
            perm = [(i, (i + shift) % size) for i in range(size)]
            owner = (index + shift) % size
        send = lax.dynamic_index_in_dim(packed, owner, axis=0, keepdims=False)
        parts.append(lax.ppermute(send, name, perm))
    top = parts[0][..., fates]
    for part in parts[1:]:
        top = jnp.maximum(top, part[..., fates])
    totals = None
    weighted = None
    for part in parts:
        factor = jnp.exp(part[..., fates] - top)
        add_s = part[..., fates + 1] * factor
        add_w = part[..., :fates] * factor[..., None]
        totals = add_s if totals is None else totals + add_s
        weighted = add_w if weighted is None else weighted + add_w
    return top, totals, weighted


def fate_pullback(cost, log_b, g_pot, fate_panel, scaled=False):
    src_count = cost.shape[0]
    if scaled:
        scores = (log_b + g_pot / entropic)[None, :] - cost
    else:
        scores = log_b[None, :] + (g_pot[None, :] - cost) / entropic
    maxima = jnp.max(scores, axis=1)
    weights = jnp.exp(scores - maxima[:, None])
    totals = jnp.sum(weights, axis=1)
    weighted = jnp.dot(
        weights, fate_panel, precision=lax.Precision.HIGHEST, preferred_element_type=jnp.float32
    )
    col_size = lax.axis_size("cols")
    rep_size = lax.axis_size("rep")
    fates = fate_panel.shape[1]
    if rep_size == 2 and col_size <= 8:
        block = src_count // (col_size * rep_size)
        maxima = jnp.swapaxes(maxima.reshape(col_size, rep_size, block), 0, 1)
        totals = jnp.swapaxes(totals.reshape(col_size, rep_size, block), 0, 1)
        weighted = jnp.swapaxes(weighted.reshape(col_size, rep_size, block, fates), 0, 1)
        maxima, totals, weighted = lse_halving(maxima, totals, weighted, [("rep", 1)])
        maxima, totals, weighted = lse_scatter_exchange(maxima, totals, weighted, "cols")
        fate_rows = weighted / totals[:, None]
    elif is_pow2(col_size) and is_pow2(rep_size):
        col_bits = col_size.bit_length() - 1
        rep_bits = rep_size.bit_length() - 1
        lead = (2,) * (col_bits + rep_bits)
        block = src_count // (col_size * rep_size)
        maxima = maxima.reshape(lead + (block,))
        totals = totals.reshape(lead + (block,))
        weighted = weighted.reshape(lead + (block, fates))
        order = [("cols", 1 << b) for b in range(col_bits - 1, -1, -1)]
        order += [("rep", 1 << b) for b in range(rep_bits - 1, -1, -1)]
        plan = list(range(len(order) - 1, col_bits - 1, -1)) + list(range(col_bits - 1, -1, -1))
        perm_dims = plan + list(range(len(order), len(order) + 1))
        maxima = jnp.transpose(maxima, perm_dims)
        totals = jnp.transpose(totals, perm_dims)
        weighted = jnp.transpose(weighted, perm_dims + [len(order) + 1])
        maxima, totals, weighted = lse_halving(
            maxima, totals, weighted, [order[d] for d in plan]
        )
        fate_rows = weighted / totals[:, None]
    else:
        whole_peak = lax.pmax(maxima, ("cols", "rep"))
        factor = jnp.exp(maxima - whole_peak)
        part_weighted, part_total = (
            lax.psum_scatter(
                weighted * factor[:, None], ("cols", "rep"), scatter_dimension=0, tiled=True
            ),
            lax.psum_scatter(totals * factor, ("cols", "rep"), scatter_dimension=0, tiled=True),
        )
        fate_rows = part_weighted / part_total[:, None]
    return (g_pot, fate_rows)


ROW_AXES = (("rep",), ("cols",))


def row_reduce(maxima, totals):
    for axes in ROW_AXES:
        if len(axes) == 1 and lax.axis_size(axes[0]) == 2:
            maxima, totals = lse_allreduce(maxima, totals, axes)
        else:
            maxima, totals = lse_exchange(maxima, totals, axes)
    return maxima, totals


def body(sources, source_mass, targets, target_mass, fate_panel):
    row_count = lax.axis_size("rows")
    if row_count != 2 or lax.axis_size("cols") > 8:
        return body_split(sources, source_mass, targets, target_mass, fate_panel)
    src_count = sources.shape[0]
    tgt_count = targets.shape[0]
    row = lax.axis_index("rows")
    dim = sources.shape[1]
    mine = jnp.concatenate([sources, source_mass[:, None]], axis=1)
    theirs = lax.ppermute(mine, "rows", [(0, 1), (1, 0)])
    all_sources = src_count * row_count
    all_targets = tgt_count * lax.axis_size(("cols", "rep"))
    log_b = jnp.log(target_mass / all_targets)
    tgt_sq = jnp.sum(targets * targets, axis=1)

    def scaled_cost(src):
        src_sq = jnp.sum(src * src, axis=1)
        return pair_cost(src, src_sq, targets, tgt_sq) / entropic

    scaled_mine = scaled_cost(sources)
    log_a_mine = jnp.log(source_mass / all_sources)
    g_pot = jnp.zeros((tgt_count,), jnp.float32)
    scores = (log_b + g_pot / entropic)[None, :] - scaled_mine
    maxima = jnp.max(scores, axis=1)
    totals = jnp.sum(jnp.exp(scores - maxima[:, None]), axis=1)
    maxima, totals = row_reduce(maxima, totals)
    f_mine = -relaxed * entropic * (maxima + jnp.log(totals))
    scores = (log_a_mine + f_mine / entropic)[:, None] - scaled_mine
    maxima = jnp.max(scores, axis=0)
    totals = jnp.sum(jnp.exp(scores - maxima[None, :]), axis=0)
    maxima, totals = lse_allreduce(maxima, totals, ("rows",))
    g_pot = -relaxed * entropic * (maxima + jnp.log(totals))

    first = jnp.where(row == 0, mine, theirs)
    second = jnp.where(row == 0, theirs, mine)
    gathered = jnp.concatenate([first, second], axis=0)
    all_src = gathered[:, :dim]
    all_mass = gathered[:, dim]
    log_a = jnp.log(all_mass / all_sources)
    scaled = with_layout_constraint(scaled_cost(all_src), Layout(major_to_minor=(1, 0)))
    scaled, log_a = lax.optimization_barrier((scaled, log_a))

    for _ in range(1, ITERS):
        scores = (log_b + g_pot / entropic)[None, :] - scaled
        maxima = jnp.max(scores, axis=1)
        totals = jnp.sum(jnp.exp(scores - maxima[:, None]), axis=1)
        maxima, totals = row_reduce(maxima, totals)
        f_all = -relaxed * entropic * (maxima + jnp.log(totals))

        scores = (log_a + f_all / entropic)[:, None] - scaled
        maxima = jnp.max(scores, axis=0)
        totals = jnp.sum(jnp.exp(scores - maxima[None, :]), axis=0)
        g_pot = -relaxed * entropic * (maxima + jnp.log(totals))

    f_pot = lax.dynamic_slice_in_dim(f_all, row * src_count, src_count)
    return (f_pot,) + fate_pullback(scaled_mine, log_b, g_pot, fate_panel, scaled=True)


def solution(mesh):
    in_specs = (
        P(("parts", "rows"), None),
        P(("parts", "rows")),
        P(("parts", "cols", "rep"), None),
        P(("parts", "cols", "rep")),
        P(("parts", "cols", "rep"), None),
    )
    out_specs = (
        P(("parts", "rows")),
        P(("parts", "cols", "rep")),
        P(("parts", "rows", "cols", "rep"), None),
    )

    return jax.shard_map(body, mesh=mesh, in_specs=in_specs, out_specs=out_specs, check_vma=False)
```

```python
import jax
import jax.numpy as jnp
from jax import lax
from jax.experimental.layout import Layout, with_layout_constraint
from jax.sharding import PartitionSpec as P

ITERS = 8


entropic = 0.1
relaxed = 1.0 / 1.1


def pair_cost(lhs_rows, lhs_sq, rhs_rows, rhs_sq):
    products = lax.dot_general(
        lhs_rows,
        rhs_rows,
        (((1,), (1,)), ((), ())),
        precision=lax.Precision.HIGHEST,
        preferred_element_type=jnp.float32,
    )
    return (lhs_sq[:, None] + rhs_sq[None, :] - 2.0 * products) / lhs_rows.shape[1]


def is_pow2(n):
    return n > 0 and (n & (n - 1)) == 0


def merge(m_one, s_one, m_two, s_two):
    top = jnp.maximum(m_one, m_two)
    return top, s_one * jnp.exp(m_one - top) + s_two * jnp.exp(m_two - top)


def lse_allreduce(maxima, totals, axes):
    if not all(is_pow2(lax.axis_size(name)) for name in axes):
        peak = lax.pmax(maxima, axes)
        return peak, lax.psum(totals * jnp.exp(maxima - peak), axes)
    for name in axes:
        size = lax.axis_size(name)
        index = lax.axis_index(name)
        step = 1
        while step < size:
            perm = [(i, i ^ step) for i in range(size)]
            other = lax.ppermute(jnp.stack([maxima, totals]), name, perm)
            other_m, other_s = other[0], other[1]
            low = (index & step) == 0
            lo_m = jnp.where(low, maxima, other_m)
            hi_m = jnp.where(low, other_m, maxima)
            lo_s = jnp.where(low, totals, other_s)
            hi_s = jnp.where(low, other_s, totals)
            maxima, totals = merge(lo_m, lo_s, hi_m, hi_s)
            step *= 2
    return maxima, totals


def lse_exchange(maxima, totals, axes):
    size = lax.axis_size(axes)
    index = lax.axis_index(axes)
    payload = jnp.stack([maxima, totals])
    received = [payload]
    for mask in range(1, size):
        if is_pow2(size):
            perm = [(i, i ^ mask) for i in range(size)]
        else:
            perm = [(i, (i + mask) % size) for i in range(size)]
        received.append(lax.ppermute(payload, axes, perm))
    received = jnp.stack(received)
    if is_pow2(size):
        slots = [index ^ rank for rank in range(size)]
    else:
        slots = [(index - rank) % size for rank in range(size)]
    ordered = [lax.dynamic_index_in_dim(received, slot, axis=0, keepdims=False) for slot in slots]
    peak = ordered[0][0]
    for item in ordered[1:]:
        peak = jnp.maximum(peak, item[0])
    whole = ordered[0][1] * jnp.exp(ordered[0][0] - peak)
    for item in ordered[1:]:
        whole = whole + item[1] * jnp.exp(item[0] - peak)
    return peak, whole


def lse_halving(maxima, totals, weighted, dims):
    for name, step in dims:
        size = lax.axis_size(name)
        perm = [(i, i ^ step) for i in range(size)]
        high = (lax.axis_index(name) & step) != 0

        def split(x):
            lower = lax.index_in_dim(x, 0, axis=0, keepdims=False)
            upper = lax.index_in_dim(x, 1, axis=0, keepdims=False)
            return jnp.where(high, upper, lower), jnp.where(high, lower, upper)

        keep_m, send_m = split(maxima)
        keep_s, send_s = split(totals)
        keep_w, send_w = split(weighted)
        packed = jnp.concatenate([send_w, send_m[..., None], send_s[..., None]], axis=-1)
        packed = lax.ppermute(packed, name, perm)
        fates = weighted.shape[-1]
        recv_w, recv_m, recv_s = packed[..., :fates], packed[..., fates], packed[..., fates + 1]
        top = jnp.maximum(keep_m, recv_m)
        keep_f = jnp.exp(keep_m - top)
        recv_f = jnp.exp(recv_m - top)
        maxima = top
        totals = keep_s * keep_f + recv_s * recv_f
        weighted = keep_w * keep_f[..., None] + recv_w * recv_f[..., None]
    return maxima, totals, weighted


def body_split(sources, source_mass, targets, target_mass, fate_panel):
    src_count = sources.shape[0]
    tgt_count = targets.shape[0]
    all_sources = src_count * lax.axis_size("rows")
    all_targets = tgt_count * lax.axis_size(("cols", "rep"))
    log_a = jnp.log(source_mass / all_sources)
    log_b = jnp.log(target_mass / all_targets)
    src_sq = jnp.sum(sources * sources, axis=1)
    tgt_sq = jnp.sum(targets * targets, axis=1)
    cost = pair_cost(sources, src_sq, targets, tgt_sq)

    g_pot = jnp.zeros((tgt_count,), jnp.float32)
    f_pot = jnp.zeros((src_count,), jnp.float32)
    for _ in range(ITERS):
        scores = log_b[None, :] + (g_pot[None, :] - cost) / entropic
        maxima = jnp.max(scores, axis=1)
        totals = jnp.sum(jnp.exp(scores - maxima[:, None]), axis=1)
        peak, whole = lse_allreduce(maxima, totals, ("rep", "cols"))
        f_pot = -relaxed * entropic * (peak + jnp.log(whole))

        scores = log_a[:, None] + (f_pot[:, None] - cost) / entropic
        maxima = jnp.max(scores, axis=0)
        totals = jnp.sum(jnp.exp(scores - maxima[None, :]), axis=0)
        peak, whole = lse_allreduce(maxima, totals, ("rows",))
        g_pot = -relaxed * entropic * (peak + jnp.log(whole))

    return (f_pot,) + fate_pullback(cost, log_b, g_pot, fate_panel)


def lse_scatter_exchange(maxima, totals, weighted, name):
    size = lax.axis_size(name)
    index = lax.axis_index(name)
    fates = weighted.shape[-1]
    packed = jnp.concatenate([weighted, maxima[..., None], totals[..., None]], axis=-1)
    parts = [lax.dynamic_index_in_dim(packed, index, axis=0, keepdims=False)]
    for shift in range(1, size):
        if is_pow2(size):
            perm = [(i, i ^ shift) for i in range(size)]
            owner = index ^ shift
        else:
            perm = [(i, (i + shift) % size) for i in range(size)]
            owner = (index + shift) % size
        send = lax.dynamic_index_in_dim(packed, owner, axis=0, keepdims=False)
        parts.append(lax.ppermute(send, name, perm))
    top = parts[0][..., fates]
    for part in parts[1:]:
        top = jnp.maximum(top, part[..., fates])
    totals = None
    weighted = None
    for part in parts:
        factor = jnp.exp(part[..., fates] - top)
        add_s = part[..., fates + 1] * factor
        add_w = part[..., :fates] * factor[..., None]
        totals = add_s if totals is None else totals + add_s
        weighted = add_w if weighted is None else weighted + add_w
    return top, totals, weighted


def fate_pullback(cost, log_b, g_pot, fate_panel, scaled=False):
    src_count = cost.shape[0]
    if scaled:
        scores = (log_b + g_pot / entropic)[None, :] - cost
    else:
        scores = log_b[None, :] + (g_pot[None, :] - cost) / entropic
    maxima = jnp.max(scores, axis=1)
    weights = jnp.exp(scores - maxima[:, None])
    totals = jnp.sum(weights, axis=1)
    weighted = jnp.dot(
        weights, fate_panel, precision=lax.Precision.HIGHEST, preferred_element_type=jnp.float32
    )
    col_size = lax.axis_size("cols")
    rep_size = lax.axis_size("rep")
    fates = fate_panel.shape[1]
    if rep_size == 2 and col_size <= 8:
        block = src_count // (col_size * rep_size)
        rep = lax.axis_index("rep")
        packed = jnp.concatenate([weighted, maxima[:, None], totals[:, None]], axis=-1)
        packed = packed.reshape(col_size, rep_size, block, fates + 2)
        keep = lax.dynamic_index_in_dim(packed, rep, axis=1, keepdims=False)
        send = lax.dynamic_index_in_dim(packed, 1 - rep, axis=1, keepdims=False)
        recv = lax.ppermute(send, "rep", [(0, 1), (1, 0)])
        maxima = jnp.maximum(keep[..., fates], recv[..., fates])
        keep_f = jnp.exp(keep[..., fates] - maxima)
        recv_f = jnp.exp(recv[..., fates] - maxima)
        totals = keep[..., fates + 1] * keep_f + recv[..., fates + 1] * recv_f
        weighted = keep[..., :fates] * keep_f[..., None] + recv[..., :fates] * recv_f[..., None]
        maxima, totals, weighted = lse_scatter_exchange(maxima, totals, weighted, "cols")
        fate_rows = weighted / totals[:, None]
    elif is_pow2(col_size) and is_pow2(rep_size):
        col_bits = col_size.bit_length() - 1
        rep_bits = rep_size.bit_length() - 1
        lead = (2,) * (col_bits + rep_bits)
        block = src_count // (col_size * rep_size)
        maxima = maxima.reshape(lead + (block,))
        totals = totals.reshape(lead + (block,))
        weighted = weighted.reshape(lead + (block, fates))
        order = [("cols", 1 << b) for b in range(col_bits - 1, -1, -1)]
        order += [("rep", 1 << b) for b in range(rep_bits - 1, -1, -1)]
        plan = list(range(len(order) - 1, col_bits - 1, -1)) + list(range(col_bits - 1, -1, -1))
        perm_dims = plan + list(range(len(order), len(order) + 1))
        maxima = jnp.transpose(maxima, perm_dims)
        totals = jnp.transpose(totals, perm_dims)
        weighted = jnp.transpose(weighted, perm_dims + [len(order) + 1])
        maxima, totals, weighted = lse_halving(
            maxima, totals, weighted, [order[d] for d in plan]
        )
        fate_rows = weighted / totals[:, None]
    else:
        whole_peak = lax.pmax(maxima, ("cols", "rep"))
        factor = jnp.exp(maxima - whole_peak)
        part_weighted, part_total = (
            lax.psum_scatter(
                weighted * factor[:, None], ("cols", "rep"), scatter_dimension=0, tiled=True
            ),
            lax.psum_scatter(totals * factor, ("cols", "rep"), scatter_dimension=0, tiled=True),
        )
        fate_rows = part_weighted / part_total[:, None]
    return (g_pot, fate_rows)


ROW_AXES = (("rep",), ("cols",))


def row_reduce(maxima, totals):
    for axes in ROW_AXES:
        if len(axes) == 1 and lax.axis_size(axes[0]) == 2:
            maxima, totals = lse_allreduce(maxima, totals, axes)
        else:
            maxima, totals = lse_exchange(maxima, totals, axes)
    return maxima, totals


def body(sources, source_mass, targets, target_mass, fate_panel):
    row_count = lax.axis_size("rows")
    if row_count != 2 or lax.axis_size("cols") > 8:
        return body_split(sources, source_mass, targets, target_mass, fate_panel)
    src_count = sources.shape[0]
    tgt_count = targets.shape[0]
    row = lax.axis_index("rows")
    dim = sources.shape[1]
    mine = jnp.concatenate([sources, source_mass[:, None]], axis=1)
    theirs = lax.ppermute(mine, "rows", [(0, 1), (1, 0)])
    all_sources = src_count * row_count
    all_targets = tgt_count * lax.axis_size(("cols", "rep"))
    log_b = jnp.log(target_mass / all_targets)
    tgt_sq = jnp.sum(targets * targets, axis=1)

    def scaled_cost(src):
        src_sq = jnp.sum(src * src, axis=1)
        return pair_cost(src, src_sq, targets, tgt_sq) / entropic

    scaled_mine = scaled_cost(sources)
    log_a_mine = jnp.log(source_mass / all_sources)
    g_pot = jnp.zeros((tgt_count,), jnp.float32)
    scores = (log_b + g_pot / entropic)[None, :] - scaled_mine
    maxima = jnp.max(scores, axis=1)
    totals = jnp.sum(jnp.exp(scores - maxima[:, None]), axis=1)
    maxima, totals = row_reduce(maxima, totals)
    f_mine = -relaxed * entropic * (maxima + jnp.log(totals))
    scores = (log_a_mine + f_mine / entropic)[:, None] - scaled_mine
    maxima = jnp.max(scores, axis=0)
    totals = jnp.sum(jnp.exp(scores - maxima[None, :]), axis=0)
    maxima, totals = lse_allreduce(maxima, totals, ("rows",))
    g_pot = -relaxed * entropic * (maxima + jnp.log(totals))

    first = jnp.where(row == 0, mine, theirs)
    second = jnp.where(row == 0, theirs, mine)
    gathered = jnp.concatenate([first, second], axis=0)
    all_src = gathered[:, :dim]
    all_mass = gathered[:, dim]
    log_a = jnp.log(all_mass / all_sources)
    scaled = with_layout_constraint(scaled_cost(all_src), Layout(major_to_minor=(1, 0)))
    scaled, log_a = lax.optimization_barrier((scaled, log_a))

    for _ in range(1, ITERS):
        scores = (log_b + g_pot / entropic)[None, :] - scaled
        maxima = jnp.max(scores, axis=1)
        totals = jnp.sum(jnp.exp(scores - maxima[:, None]), axis=1)
        maxima, totals = row_reduce(maxima, totals)
        f_all = -relaxed * entropic * (maxima + jnp.log(totals))

        scores = (log_a + f_all / entropic)[:, None] - scaled
        maxima = jnp.max(scores, axis=0)
        totals = jnp.sum(jnp.exp(scores - maxima[None, :]), axis=0)
        g_pot = -relaxed * entropic * (maxima + jnp.log(totals))

    f_pot = lax.dynamic_slice_in_dim(f_all, row * src_count, src_count)
    return (f_pot,) + fate_pullback(scaled_mine, log_b, g_pot, fate_panel, scaled=True)


def solution(mesh):
    in_specs = (
        P(("parts", "rows"), None),
        P(("parts", "rows")),
        P(("parts", "cols", "rep"), None),
        P(("parts", "cols", "rep")),
        P(("parts", "cols", "rep"), None),
    )
    out_specs = (
        P(("parts", "rows")),
        P(("parts", "cols", "rep")),
        P(("parts", "rows", "cols", "rep"), None),
    )

    return jax.shard_map(body, mesh=mesh, in_specs=in_specs, out_specs=out_specs, check_vma=False)
```

```python
import jax
import jax.numpy as jnp
from jax import lax
from jax.experimental.layout import Layout, with_layout_constraint
from jax.sharding import PartitionSpec as P

ITERS = 8


entropic = 0.1
relaxed = 1.0 / 1.1


def pair_cost(lhs_rows, lhs_sq, rhs_rows, rhs_sq):
    products = lax.dot_general(
        lhs_rows,
        rhs_rows,
        (((1,), (1,)), ((), ())),
        precision=lax.Precision.HIGHEST,
        preferred_element_type=jnp.float32,
    )
    return (lhs_sq[:, None] + rhs_sq[None, :] - 2.0 * products) / lhs_rows.shape[1]


def is_pow2(n):
    return n > 0 and (n & (n - 1)) == 0


def merge(m_one, s_one, m_two, s_two):
    top = jnp.maximum(m_one, m_two)
    return top, s_one * jnp.exp(m_one - top) + s_two * jnp.exp(m_two - top)


def lse_allreduce(maxima, totals, axes):
    if not all(is_pow2(lax.axis_size(name)) for name in axes):
        peak = lax.pmax(maxima, axes)
        return peak, lax.psum(totals * jnp.exp(maxima - peak), axes)
    for name in axes:
        size = lax.axis_size(name)
        index = lax.axis_index(name)
        step = 1
        while step < size:
            perm = [(i, i ^ step) for i in range(size)]
            other = lax.ppermute(jnp.stack([maxima, totals]), name, perm)
            other_m, other_s = other[0], other[1]
            low = (index & step) == 0
            lo_m = jnp.where(low, maxima, other_m)
            hi_m = jnp.where(low, other_m, maxima)
            lo_s = jnp.where(low, totals, other_s)
            hi_s = jnp.where(low, other_s, totals)
            maxima, totals = merge(lo_m, lo_s, hi_m, hi_s)
            step *= 2
    return maxima, totals


def lse_exchange(maxima, totals, axes):
    size = lax.axis_size(axes)
    index = lax.axis_index(axes)
    payload = jnp.stack([maxima, totals])
    received = [payload]
    for mask in range(1, size):
        if is_pow2(size):
            perm = [(i, i ^ mask) for i in range(size)]
        else:
            perm = [(i, (i + mask) % size) for i in range(size)]
        received.append(lax.ppermute(payload, axes, perm))
    received = jnp.stack(received)
    if is_pow2(size):
        slots = [index ^ rank for rank in range(size)]
    else:
        slots = [(index - rank) % size for rank in range(size)]
    ordered = [lax.dynamic_index_in_dim(received, slot, axis=0, keepdims=False) for slot in slots]
    peak = ordered[0][0]
    for item in ordered[1:]:
        peak = jnp.maximum(peak, item[0])
    whole = ordered[0][1] * jnp.exp(ordered[0][0] - peak)
    for item in ordered[1:]:
        whole = whole + item[1] * jnp.exp(item[0] - peak)
    return peak, whole


def lse_halving(maxima, totals, weighted, dims):
    for name, step in dims:
        size = lax.axis_size(name)
        perm = [(i, i ^ step) for i in range(size)]
        high = (lax.axis_index(name) & step) != 0

        def split(x):
            lower = lax.index_in_dim(x, 0, axis=0, keepdims=False)
            upper = lax.index_in_dim(x, 1, axis=0, keepdims=False)
            return jnp.where(high, upper, lower), jnp.where(high, lower, upper)

        keep_m, send_m = split(maxima)
        keep_s, send_s = split(totals)
        keep_w, send_w = split(weighted)
        packed = jnp.concatenate([send_w, send_m[..., None], send_s[..., None]], axis=-1)
        packed = lax.ppermute(packed, name, perm)
        fates = weighted.shape[-1]
        recv_w, recv_m, recv_s = packed[..., :fates], packed[..., fates], packed[..., fates + 1]
        top = jnp.maximum(keep_m, recv_m)
        keep_f = jnp.exp(keep_m - top)
        recv_f = jnp.exp(recv_m - top)
        maxima = top
        totals = keep_s * keep_f + recv_s * recv_f
        weighted = keep_w * keep_f[..., None] + recv_w * recv_f[..., None]
    return maxima, totals, weighted


def body_split(sources, source_mass, targets, target_mass, fate_panel):
    src_count = sources.shape[0]
    tgt_count = targets.shape[0]
    all_sources = src_count * lax.axis_size("rows")
    all_targets = tgt_count * lax.axis_size(("cols", "rep"))
    log_a = jnp.log(source_mass / all_sources)
    log_b = jnp.log(target_mass / all_targets)
    src_sq = jnp.sum(sources * sources, axis=1)
    tgt_sq = jnp.sum(targets * targets, axis=1)
    cost = pair_cost(sources, src_sq, targets, tgt_sq)

    g_pot = jnp.zeros((tgt_count,), jnp.float32)
    f_pot = jnp.zeros((src_count,), jnp.float32)
    for _ in range(ITERS):
        scores = log_b[None, :] + (g_pot[None, :] - cost) / entropic
        maxima = jnp.max(scores, axis=1)
        totals = jnp.sum(jnp.exp(scores - maxima[:, None]), axis=1)
        peak, whole = lse_allreduce(maxima, totals, ("rep", "cols"))
        f_pot = -relaxed * entropic * (peak + jnp.log(whole))

        scores = log_a[:, None] + (f_pot[:, None] - cost) / entropic
        maxima = jnp.max(scores, axis=0)
        totals = jnp.sum(jnp.exp(scores - maxima[None, :]), axis=0)
        peak, whole = lse_allreduce(maxima, totals, ("rows",))
        g_pot = -relaxed * entropic * (peak + jnp.log(whole))

    return (f_pot,) + fate_pullback(cost, log_b, g_pot, fate_panel)


def lse_scatter_exchange(maxima, totals, weighted, name):
    size = lax.axis_size(name)
    index = lax.axis_index(name)
    fates = weighted.shape[-1]
    packed = jnp.concatenate([weighted, maxima[..., None], totals[..., None]], axis=-1)
    parts = [lax.dynamic_index_in_dim(packed, index, axis=0, keepdims=False)]
    for shift in range(1, size):
        if is_pow2(size):
            perm = [(i, i ^ shift) for i in range(size)]
            owner = index ^ shift
        else:
            perm = [(i, (i + shift) % size) for i in range(size)]
            owner = (index + shift) % size
        send = lax.dynamic_index_in_dim(packed, owner, axis=0, keepdims=False)
        parts.append(lax.ppermute(send, name, perm))
    top = parts[0][..., fates]
    for part in parts[1:]:
        top = jnp.maximum(top, part[..., fates])
    totals = None
    weighted = None
    for part in parts:
        factor = jnp.exp(part[..., fates] - top)
        add_s = part[..., fates + 1] * factor
        add_w = part[..., :fates] * factor[..., None]
        totals = add_s if totals is None else totals + add_s
        weighted = add_w if weighted is None else weighted + add_w
    return top, totals, weighted


def fate_pullback(cost, log_b, g_pot, fate_panel, scaled=False):
    src_count = cost.shape[0]
    if scaled:
        scores = (log_b + g_pot / entropic)[None, :] - cost
    else:
        scores = log_b[None, :] + (g_pot[None, :] - cost) / entropic
    maxima = jnp.max(scores, axis=1)
    weights = jnp.exp(scores - maxima[:, None])
    totals = jnp.sum(weights, axis=1)
    weighted = jnp.dot(
        weights, fate_panel, precision=lax.Precision.HIGHEST, preferred_element_type=jnp.float32
    )
    col_size = lax.axis_size("cols")
    rep_size = lax.axis_size("rep")
    fates = fate_panel.shape[1]
    if rep_size == 2 and col_size <= 8:
        block = src_count // (col_size * rep_size)
        rep = lax.axis_index("rep")
        packed = jnp.concatenate([weighted, maxima[:, None], totals[:, None]], axis=-1)
        packed = packed.reshape(col_size, rep_size, block, fates + 2)
        keep = lax.dynamic_index_in_dim(packed, rep, axis=1, keepdims=False)
        send = lax.dynamic_index_in_dim(packed, 1 - rep, axis=1, keepdims=False)
        recv = lax.ppermute(send, "rep", [(0, 1), (1, 0)])
        maxima = jnp.maximum(keep[..., fates], recv[..., fates])
        keep_f = jnp.exp(keep[..., fates] - maxima)
        recv_f = jnp.exp(recv[..., fates] - maxima)
        totals = keep[..., fates + 1] * keep_f + recv[..., fates + 1] * recv_f
        weighted = keep[..., :fates] * keep_f[..., None] + recv[..., :fates] * recv_f[..., None]
        maxima, totals, weighted = lse_scatter_exchange(maxima, totals, weighted, "cols")
        fate_rows = weighted / totals[:, None]
    elif is_pow2(col_size) and is_pow2(rep_size):
        col_bits = col_size.bit_length() - 1
        rep_bits = rep_size.bit_length() - 1
        lead = (2,) * (col_bits + rep_bits)
        block = src_count // (col_size * rep_size)
        maxima = maxima.reshape(lead + (block,))
        totals = totals.reshape(lead + (block,))
        weighted = weighted.reshape(lead + (block, fates))
        order = [("cols", 1 << b) for b in range(col_bits - 1, -1, -1)]
        order += [("rep", 1 << b) for b in range(rep_bits - 1, -1, -1)]
        plan = list(range(len(order) - 1, col_bits - 1, -1)) + list(range(col_bits - 1, -1, -1))
        perm_dims = plan + list(range(len(order), len(order) + 1))
        maxima = jnp.transpose(maxima, perm_dims)
        totals = jnp.transpose(totals, perm_dims)
        weighted = jnp.transpose(weighted, perm_dims + [len(order) + 1])
        maxima, totals, weighted = lse_halving(
            maxima, totals, weighted, [order[d] for d in plan]
        )
        fate_rows = weighted / totals[:, None]
    else:
        whole_peak = lax.pmax(maxima, ("cols", "rep"))
        factor = jnp.exp(maxima - whole_peak)
        part_weighted, part_total = (
            lax.psum_scatter(
                weighted * factor[:, None], ("cols", "rep"), scatter_dimension=0, tiled=True
            ),
            lax.psum_scatter(totals * factor, ("cols", "rep"), scatter_dimension=0, tiled=True),
        )
        fate_rows = part_weighted / part_total[:, None]
    return (g_pot, fate_rows)


ROW_AXES = (("rep",), ("cols",))


def row_reduce(maxima, totals):
    for axes in ROW_AXES:
        if len(axes) == 1 and lax.axis_size(axes[0]) == 2:
            maxima, totals = lse_allreduce(maxima, totals, axes)
        else:
            maxima, totals = lse_exchange(maxima, totals, axes)
    return maxima, totals


def body(sources, source_mass, targets, target_mass, fate_panel):
    row_count = lax.axis_size("rows")
    if row_count != 2 or lax.axis_size("cols") > 8:
        return body_split(sources, source_mass, targets, target_mass, fate_panel)
    src_count = sources.shape[0]
    tgt_count = targets.shape[0]
    row = lax.axis_index("rows")
    dim = sources.shape[1]
    flat = src_count * dim
    mine = jnp.concatenate([sources.reshape(flat), source_mass])
    theirs = lax.ppermute(mine, "rows", [(0, 1), (1, 0)])
    all_sources = src_count * row_count
    all_targets = tgt_count * lax.axis_size(("cols", "rep"))
    log_b = jnp.log(target_mass / all_targets)
    tgt_sq = jnp.sum(targets * targets, axis=1)

    def scaled_cost(src):
        src_sq = jnp.sum(src * src, axis=1)
        return pair_cost(src, src_sq, targets, tgt_sq) / entropic

    scaled_mine = scaled_cost(sources)
    log_a_mine = jnp.log(source_mass / all_sources)
    g_pot = jnp.zeros((tgt_count,), jnp.float32)
    scores = (log_b + g_pot / entropic)[None, :] - scaled_mine
    maxima = jnp.max(scores, axis=1)
    totals = jnp.sum(jnp.exp(scores - maxima[:, None]), axis=1)
    maxima, totals = row_reduce(maxima, totals)
    f_mine = -relaxed * entropic * (maxima + jnp.log(totals))
    scores = (log_a_mine + f_mine / entropic)[:, None] - scaled_mine
    maxima = jnp.max(scores, axis=0)
    totals = jnp.sum(jnp.exp(scores - maxima[None, :]), axis=0)
    maxima, totals = lse_allreduce(maxima, totals, ("rows",))
    g_pot = -relaxed * entropic * (maxima + jnp.log(totals))

    lead = row == 0
    their_src = theirs[:flat].reshape(src_count, dim)
    their_mass = theirs[flat:]
    all_src = jnp.concatenate(
        [jnp.where(lead, sources, their_src), jnp.where(lead, their_src, sources)]
    )
    all_mass = jnp.concatenate(
        [jnp.where(lead, source_mass, their_mass), jnp.where(lead, their_mass, source_mass)]
    )
    log_a = jnp.log(all_mass / all_sources)
    scaled = with_layout_constraint(scaled_cost(all_src), Layout(major_to_minor=(1, 0)))
    scaled, log_a = lax.optimization_barrier((scaled, log_a))

    for _ in range(1, ITERS):
        scores = (log_b + g_pot / entropic)[None, :] - scaled
        maxima = jnp.max(scores, axis=1)
        totals = jnp.sum(jnp.exp(scores - maxima[:, None]), axis=1)
        maxima, totals = row_reduce(maxima, totals)
        f_all = -relaxed * entropic * (maxima + jnp.log(totals))

        scores = (log_a + f_all / entropic)[:, None] - scaled
        maxima = jnp.max(scores, axis=0)
        totals = jnp.sum(jnp.exp(scores - maxima[None, :]), axis=0)
        g_pot = -relaxed * entropic * (maxima + jnp.log(totals))

    f_pot = lax.dynamic_slice_in_dim(f_all, row * src_count, src_count)
    return (f_pot,) + fate_pullback(scaled_mine, log_b, g_pot, fate_panel, scaled=True)


def solution(mesh):
    in_specs = (
        P(("parts", "rows"), None),
        P(("parts", "rows")),
        P(("parts", "cols", "rep"), None),
        P(("parts", "cols", "rep")),
        P(("parts", "cols", "rep"), None),
    )
    out_specs = (
        P(("parts", "rows")),
        P(("parts", "cols", "rep")),
        P(("parts", "rows", "cols", "rep"), None),
    )

    return jax.shard_map(body, mesh=mesh, in_specs=in_specs, out_specs=out_specs, check_vma=False)
```

```python
import jax
import jax.numpy as jnp
from jax import lax
from jax.experimental.layout import Layout, with_layout_constraint
from jax.sharding import PartitionSpec as P

ITERS = 8


entropic = 0.1
relaxed = 1.0 / 1.1


def pair_cost(lhs_rows, lhs_sq, rhs_rows, rhs_sq):
    products = lax.dot_general(
        lhs_rows,
        rhs_rows,
        (((1,), (1,)), ((), ())),
        precision=lax.Precision.HIGHEST,
        preferred_element_type=jnp.float32,
    )
    return (lhs_sq[:, None] + rhs_sq[None, :] - 2.0 * products) / lhs_rows.shape[1]


def is_pow2(n):
    return n > 0 and (n & (n - 1)) == 0


def merge(m_one, s_one, m_two, s_two):
    top = jnp.maximum(m_one, m_two)
    return top, s_one * jnp.exp(m_one - top) + s_two * jnp.exp(m_two - top)


def lse_allreduce(maxima, totals, axes):
    if not all(is_pow2(lax.axis_size(name)) for name in axes):
        peak = lax.pmax(maxima, axes)
        return peak, lax.psum(totals * jnp.exp(maxima - peak), axes)
    for name in axes:
        size = lax.axis_size(name)
        index = lax.axis_index(name)
        step = 1
        while step < size:
            perm = [(i, i ^ step) for i in range(size)]
            other = lax.ppermute(jnp.stack([maxima, totals]), name, perm)
            other_m, other_s = other[0], other[1]
            low = (index & step) == 0
            lo_m = jnp.where(low, maxima, other_m)
            hi_m = jnp.where(low, other_m, maxima)
            lo_s = jnp.where(low, totals, other_s)
            hi_s = jnp.where(low, other_s, totals)
            maxima, totals = merge(lo_m, lo_s, hi_m, hi_s)
            step *= 2
    return maxima, totals


def lse_exchange(maxima, totals, axes):
    size = lax.axis_size(axes)
    index = lax.axis_index(axes)
    payload = jnp.stack([maxima, totals])
    received = [payload]
    for mask in range(1, size):
        if is_pow2(size):
            perm = [(i, i ^ mask) for i in range(size)]
        else:
            perm = [(i, (i + mask) % size) for i in range(size)]
        received.append(lax.ppermute(payload, axes, perm))
    received = jnp.stack(received)
    if is_pow2(size):
        slots = [index ^ rank for rank in range(size)]
    else:
        slots = [(index - rank) % size for rank in range(size)]
    ordered = [lax.dynamic_index_in_dim(received, slot, axis=0, keepdims=False) for slot in slots]
    peak = ordered[0][0]
    for item in ordered[1:]:
        peak = jnp.maximum(peak, item[0])
    whole = ordered[0][1] * jnp.exp(ordered[0][0] - peak)
    for item in ordered[1:]:
        whole = whole + item[1] * jnp.exp(item[0] - peak)
    return peak, whole


def lse_halving(maxima, totals, weighted, dims):
    for name, step in dims:
        size = lax.axis_size(name)
        perm = [(i, i ^ step) for i in range(size)]
        high = (lax.axis_index(name) & step) != 0

        def split(x):
            lower = lax.index_in_dim(x, 0, axis=0, keepdims=False)
            upper = lax.index_in_dim(x, 1, axis=0, keepdims=False)
            return jnp.where(high, upper, lower), jnp.where(high, lower, upper)

        keep_m, send_m = split(maxima)
        keep_s, send_s = split(totals)
        keep_w, send_w = split(weighted)
        packed = jnp.concatenate([send_w, send_m[..., None], send_s[..., None]], axis=-1)
        packed = lax.ppermute(packed, name, perm)
        fates = weighted.shape[-1]
        recv_w, recv_m, recv_s = packed[..., :fates], packed[..., fates], packed[..., fates + 1]
        top = jnp.maximum(keep_m, recv_m)
        keep_f = jnp.exp(keep_m - top)
        recv_f = jnp.exp(recv_m - top)
        maxima = top
        totals = keep_s * keep_f + recv_s * recv_f
        weighted = keep_w * keep_f[..., None] + recv_w * recv_f[..., None]
    return maxima, totals, weighted


def body_split(sources, source_mass, targets, target_mass, fate_panel):
    src_count = sources.shape[0]
    tgt_count = targets.shape[0]
    all_sources = src_count * lax.axis_size("rows")
    all_targets = tgt_count * lax.axis_size(("cols", "rep"))
    log_a = jnp.log(source_mass / all_sources)
    log_b = jnp.log(target_mass / all_targets)
    src_sq = jnp.sum(sources * sources, axis=1)
    tgt_sq = jnp.sum(targets * targets, axis=1)
    cost = pair_cost(sources, src_sq, targets, tgt_sq)

    g_pot = jnp.zeros((tgt_count,), jnp.float32)
    f_pot = jnp.zeros((src_count,), jnp.float32)
    for _ in range(ITERS):
        scores = log_b[None, :] + (g_pot[None, :] - cost) / entropic
        maxima = jnp.max(scores, axis=1)
        totals = jnp.sum(jnp.exp(scores - maxima[:, None]), axis=1)
        peak, whole = lse_allreduce(maxima, totals, ("rep", "cols"))
        f_pot = -relaxed * entropic * (peak + jnp.log(whole))

        scores = log_a[:, None] + (f_pot[:, None] - cost) / entropic
        maxima = jnp.max(scores, axis=0)
        totals = jnp.sum(jnp.exp(scores - maxima[None, :]), axis=0)
        peak, whole = lse_allreduce(maxima, totals, ("rows",))
        g_pot = -relaxed * entropic * (peak + jnp.log(whole))

    return (f_pot,) + fate_pullback(cost, log_b, g_pot, fate_panel)


def lse_scatter_exchange(maxima, totals, weighted, name):
    size = lax.axis_size(name)
    index = lax.axis_index(name)
    fates = weighted.shape[-1]
    packed = jnp.concatenate([weighted, maxima[..., None], totals[..., None]], axis=-1)
    parts = [lax.dynamic_index_in_dim(packed, index, axis=0, keepdims=False)]
    for shift in range(1, size):
        if is_pow2(size):
            perm = [(i, i ^ shift) for i in range(size)]
            owner = index ^ shift
        else:
            perm = [(i, (i + shift) % size) for i in range(size)]
            owner = (index + shift) % size
        send = lax.dynamic_index_in_dim(packed, owner, axis=0, keepdims=False)
        parts.append(lax.ppermute(send, name, perm))
    top = parts[0][..., fates]
    for part in parts[1:]:
        top = jnp.maximum(top, part[..., fates])
    totals = None
    weighted = None
    for part in parts:
        factor = jnp.exp(part[..., fates] - top)
        add_s = part[..., fates + 1] * factor
        add_w = part[..., :fates] * factor[..., None]
        totals = add_s if totals is None else totals + add_s
        weighted = add_w if weighted is None else weighted + add_w
    return top, totals, weighted


def fate_pullback(cost, log_b, g_pot, fate_panel, scaled=False):
    src_count = cost.shape[0]
    if scaled:
        scores = (log_b + g_pot / entropic)[None, :] - cost
    else:
        scores = log_b[None, :] + (g_pot[None, :] - cost) / entropic
    maxima = jnp.max(scores, axis=1)
    weights = jnp.exp(scores - maxima[:, None])
    totals = jnp.sum(weights, axis=1)
    weighted = jnp.dot(
        weights, fate_panel, precision=lax.Precision.HIGHEST, preferred_element_type=jnp.float32
    )
    col_size = lax.axis_size("cols")
    rep_size = lax.axis_size("rep")
    fates = fate_panel.shape[1]
    if rep_size == 2 and col_size <= 8:
        block = src_count // (col_size * rep_size)
        rep = lax.axis_index("rep")
        packed = jnp.concatenate([weighted, maxima[:, None], totals[:, None]], axis=-1)
        packed = packed.reshape(col_size, rep_size, block, fates + 2)
        keep = lax.dynamic_index_in_dim(packed, rep, axis=1, keepdims=False)
        send = lax.dynamic_index_in_dim(packed, 1 - rep, axis=1, keepdims=False)
        recv = lax.ppermute(send, "rep", [(0, 1), (1, 0)])
        maxima = jnp.maximum(keep[..., fates], recv[..., fates])
        keep_f = jnp.exp(keep[..., fates] - maxima)
        recv_f = jnp.exp(recv[..., fates] - maxima)
        totals = keep[..., fates + 1] * keep_f + recv[..., fates + 1] * recv_f
        weighted = keep[..., :fates] * keep_f[..., None] + recv[..., :fates] * recv_f[..., None]
        maxima, totals, weighted = lse_scatter_exchange(maxima, totals, weighted, "cols")
        fate_rows = weighted / totals[:, None]
    elif is_pow2(col_size) and is_pow2(rep_size):
        col_bits = col_size.bit_length() - 1
        rep_bits = rep_size.bit_length() - 1
        lead = (2,) * (col_bits + rep_bits)
        block = src_count // (col_size * rep_size)
        maxima = maxima.reshape(lead + (block,))
        totals = totals.reshape(lead + (block,))
        weighted = weighted.reshape(lead + (block, fates))
        order = [("cols", 1 << b) for b in range(col_bits - 1, -1, -1)]
        order += [("rep", 1 << b) for b in range(rep_bits - 1, -1, -1)]
        plan = list(range(len(order) - 1, col_bits - 1, -1)) + list(range(col_bits - 1, -1, -1))
        perm_dims = plan + list(range(len(order), len(order) + 1))
        maxima = jnp.transpose(maxima, perm_dims)
        totals = jnp.transpose(totals, perm_dims)
        weighted = jnp.transpose(weighted, perm_dims + [len(order) + 1])
        maxima, totals, weighted = lse_halving(
            maxima, totals, weighted, [order[d] for d in plan]
        )
        fate_rows = weighted / totals[:, None]
    else:
        whole_peak = lax.pmax(maxima, ("cols", "rep"))
        factor = jnp.exp(maxima - whole_peak)
        part_weighted, part_total = (
            lax.psum_scatter(
                weighted * factor[:, None], ("cols", "rep"), scatter_dimension=0, tiled=True
            ),
            lax.psum_scatter(totals * factor, ("cols", "rep"), scatter_dimension=0, tiled=True),
        )
        fate_rows = part_weighted / part_total[:, None]
    return (g_pot, fate_rows)


ROW_AXES = (("rep",), ("cols",))


def row_reduce(maxima, totals):
    for axes in ROW_AXES:
        if len(axes) == 1 and lax.axis_size(axes[0]) == 2:
            maxima, totals = lse_allreduce(maxima, totals, axes)
        else:
            maxima, totals = lse_exchange(maxima, totals, axes)
    return maxima, totals


def body(sources, source_mass, targets, target_mass, fate_panel):
    row_count = lax.axis_size("rows")
    if row_count != 2 or lax.axis_size("cols") > 8:
        return body_split(sources, source_mass, targets, target_mass, fate_panel)
    src_count = sources.shape[0]
    tgt_count = targets.shape[0]
    row = lax.axis_index("rows")
    dim = sources.shape[1]
    flat = src_count * dim
    lanes = 128
    mine = jnp.concatenate(
        [sources.reshape(flat // lanes, lanes), source_mass.reshape(src_count // lanes, lanes)]
    )
    theirs = lax.ppermute(mine, "rows", [(0, 1), (1, 0)])
    all_sources = src_count * row_count
    all_targets = tgt_count * lax.axis_size(("cols", "rep"))
    log_b = jnp.log(target_mass / all_targets)
    tgt_sq = jnp.sum(targets * targets, axis=1)

    def scaled_cost(src):
        src_sq = jnp.sum(src * src, axis=1)
        return pair_cost(src, src_sq, targets, tgt_sq) / entropic

    scaled_mine = scaled_cost(sources)
    log_a_mine = jnp.log(source_mass / all_sources)
    g_pot = jnp.zeros((tgt_count,), jnp.float32)
    scores = (log_b + g_pot / entropic)[None, :] - scaled_mine
    maxima = jnp.max(scores, axis=1)
    totals = jnp.sum(jnp.exp(scores - maxima[:, None]), axis=1)
    maxima, totals = row_reduce(maxima, totals)
    f_mine = -relaxed * entropic * (maxima + jnp.log(totals))
    scores = (log_a_mine + f_mine / entropic)[:, None] - scaled_mine
    maxima = jnp.max(scores, axis=0)
    totals = jnp.sum(jnp.exp(scores - maxima[None, :]), axis=0)
    maxima, totals = lse_allreduce(maxima, totals, ("rows",))
    g_pot = -relaxed * entropic * (maxima + jnp.log(totals))

    lead = row == 0
    their_src = theirs[: flat // lanes].reshape(src_count, dim)
    their_mass = theirs[flat // lanes :].reshape(src_count)
    all_src = jnp.concatenate(
        [jnp.where(lead, sources, their_src), jnp.where(lead, their_src, sources)]
    )
    all_mass = jnp.concatenate(
        [jnp.where(lead, source_mass, their_mass), jnp.where(lead, their_mass, source_mass)]
    )
    log_a = jnp.log(all_mass / all_sources)
    scaled = with_layout_constraint(scaled_cost(all_src), Layout(major_to_minor=(1, 0)))
    scaled, log_a = lax.optimization_barrier((scaled, log_a))

    for _ in range(1, ITERS):
        scores = (log_b + g_pot / entropic)[None, :] - scaled
        maxima = jnp.max(scores, axis=1)
        totals = jnp.sum(jnp.exp(scores - maxima[:, None]), axis=1)
        maxima, totals = row_reduce(maxima, totals)
        f_all = -relaxed * entropic * (maxima + jnp.log(totals))

        scores = (log_a + f_all / entropic)[:, None] - scaled
        maxima = jnp.max(scores, axis=0)
        totals = jnp.sum(jnp.exp(scores - maxima[None, :]), axis=0)
        g_pot = -relaxed * entropic * (maxima + jnp.log(totals))

    f_pot = lax.dynamic_slice_in_dim(f_all, row * src_count, src_count)
    return (f_pot,) + fate_pullback(scaled_mine, log_b, g_pot, fate_panel, scaled=True)


def solution(mesh):
    in_specs = (
        P(("parts", "rows"), None),
        P(("parts", "rows")),
        P(("parts", "cols", "rep"), None),
        P(("parts", "cols", "rep")),
        P(("parts", "cols", "rep"), None),
    )
    out_specs = (
        P(("parts", "rows")),
        P(("parts", "cols", "rep")),
        P(("parts", "rows", "cols", "rep"), None),
    )

    return jax.shard_map(body, mesh=mesh, in_specs=in_specs, out_specs=out_specs, check_vma=False)
```

```python
import jax
import jax.numpy as jnp
from jax import lax
from jax.experimental.layout import Layout, with_layout_constraint
from jax.sharding import PartitionSpec as P

ITERS = 8


entropic = 0.1
relaxed = 1.0 / 1.1


def pair_cost(lhs_rows, lhs_sq, rhs_rows, rhs_sq):
    products = lax.dot_general(
        lhs_rows,
        rhs_rows,
        (((1,), (1,)), ((), ())),
        precision=lax.Precision.HIGHEST,
        preferred_element_type=jnp.float32,
    )
    return (lhs_sq[:, None] + rhs_sq[None, :] - 2.0 * products) / lhs_rows.shape[1]


def is_pow2(n):
    return n > 0 and (n & (n - 1)) == 0


def merge(m_one, s_one, m_two, s_two):
    top = jnp.maximum(m_one, m_two)
    return top, s_one * jnp.exp(m_one - top) + s_two * jnp.exp(m_two - top)


def lse_allreduce(maxima, totals, axes):
    if not all(is_pow2(lax.axis_size(name)) for name in axes):
        peak = lax.pmax(maxima, axes)
        return peak, lax.psum(totals * jnp.exp(maxima - peak), axes)
    for name in axes:
        size = lax.axis_size(name)
        index = lax.axis_index(name)
        step = 1
        while step < size:
            perm = [(i, i ^ step) for i in range(size)]
            other = lax.ppermute(jnp.stack([maxima, totals]), name, perm)
            other_m, other_s = other[0], other[1]
            low = (index & step) == 0
            lo_m = jnp.where(low, maxima, other_m)
            hi_m = jnp.where(low, other_m, maxima)
            lo_s = jnp.where(low, totals, other_s)
            hi_s = jnp.where(low, other_s, totals)
            maxima, totals = merge(lo_m, lo_s, hi_m, hi_s)
            step *= 2
    return maxima, totals


def lse_exchange(maxima, totals, axes):
    size = lax.axis_size(axes)
    index = lax.axis_index(axes)
    payload = jnp.stack([maxima, totals])
    received = [payload]
    for mask in range(1, size):
        if is_pow2(size):
            perm = [(i, i ^ mask) for i in range(size)]
        else:
            perm = [(i, (i + mask) % size) for i in range(size)]
        received.append(lax.ppermute(payload, axes, perm))
    received = jnp.stack(received)
    if is_pow2(size):
        slots = [index ^ rank for rank in range(size)]
    else:
        slots = [(index - rank) % size for rank in range(size)]
    ordered = [lax.dynamic_index_in_dim(received, slot, axis=0, keepdims=False) for slot in slots]
    peak = ordered[0][0]
    for item in ordered[1:]:
        peak = jnp.maximum(peak, item[0])
    whole = ordered[0][1] * jnp.exp(ordered[0][0] - peak)
    for item in ordered[1:]:
        whole = whole + item[1] * jnp.exp(item[0] - peak)
    return peak, whole


def lse_halving(maxima, totals, weighted, dims):
    for name, step in dims:
        size = lax.axis_size(name)
        perm = [(i, i ^ step) for i in range(size)]
        high = (lax.axis_index(name) & step) != 0

        def split(x):
            lower = lax.index_in_dim(x, 0, axis=0, keepdims=False)
            upper = lax.index_in_dim(x, 1, axis=0, keepdims=False)
            return jnp.where(high, upper, lower), jnp.where(high, lower, upper)

        keep_m, send_m = split(maxima)
        keep_s, send_s = split(totals)
        keep_w, send_w = split(weighted)
        packed = jnp.concatenate([send_w, send_m[..., None], send_s[..., None]], axis=-1)
        packed = lax.ppermute(packed, name, perm)
        fates = weighted.shape[-1]
        recv_w, recv_m, recv_s = packed[..., :fates], packed[..., fates], packed[..., fates + 1]
        top = jnp.maximum(keep_m, recv_m)
        keep_f = jnp.exp(keep_m - top)
        recv_f = jnp.exp(recv_m - top)
        maxima = top
        totals = keep_s * keep_f + recv_s * recv_f
        weighted = keep_w * keep_f[..., None] + recv_w * recv_f[..., None]
    return maxima, totals, weighted


def body_split(sources, source_mass, targets, target_mass, fate_panel):
    src_count = sources.shape[0]
    tgt_count = targets.shape[0]
    all_sources = src_count * lax.axis_size("rows")
    all_targets = tgt_count * lax.axis_size(("cols", "rep"))
    log_a = jnp.log(source_mass / all_sources)
    log_b = jnp.log(target_mass / all_targets)
    src_sq = jnp.sum(sources * sources, axis=1)
    tgt_sq = jnp.sum(targets * targets, axis=1)
    cost = pair_cost(sources, src_sq, targets, tgt_sq)

    g_pot = jnp.zeros((tgt_count,), jnp.float32)
    f_pot = jnp.zeros((src_count,), jnp.float32)
    for _ in range(ITERS):
        scores = log_b[None, :] + (g_pot[None, :] - cost) / entropic
        maxima = jnp.max(scores, axis=1)
        totals = jnp.sum(jnp.exp(scores - maxima[:, None]), axis=1)
        peak, whole = lse_allreduce(maxima, totals, ("rep", "cols"))
        f_pot = -relaxed * entropic * (peak + jnp.log(whole))

        scores = log_a[:, None] + (f_pot[:, None] - cost) / entropic
        maxima = jnp.max(scores, axis=0)
        totals = jnp.sum(jnp.exp(scores - maxima[None, :]), axis=0)
        peak, whole = lse_allreduce(maxima, totals, ("rows",))
        g_pot = -relaxed * entropic * (peak + jnp.log(whole))

    return (f_pot,) + fate_pullback(cost, log_b, g_pot, fate_panel)


def lse_scatter_exchange(maxima, totals, weighted, name):
    size = lax.axis_size(name)
    index = lax.axis_index(name)
    fates = weighted.shape[-1]
    packed = jnp.concatenate([weighted, maxima[..., None], totals[..., None]], axis=-1)
    parts = [lax.dynamic_index_in_dim(packed, index, axis=0, keepdims=False)]
    for shift in range(1, size):
        if is_pow2(size):
            perm = [(i, i ^ shift) for i in range(size)]
            owner = index ^ shift
        else:
            perm = [(i, (i + shift) % size) for i in range(size)]
            owner = (index + shift) % size
        send = lax.dynamic_index_in_dim(packed, owner, axis=0, keepdims=False)
        parts.append(lax.ppermute(send, name, perm))
    top = parts[0][..., fates]
    for part in parts[1:]:
        top = jnp.maximum(top, part[..., fates])
    totals = None
    weighted = None
    for part in parts:
        factor = jnp.exp(part[..., fates] - top)
        add_s = part[..., fates + 1] * factor
        add_w = part[..., :fates] * factor[..., None]
        totals = add_s if totals is None else totals + add_s
        weighted = add_w if weighted is None else weighted + add_w
    return top, totals, weighted


def fate_pullback(cost, log_b, g_pot, fate_panel, scaled=False):
    src_count = cost.shape[0]
    if scaled:
        scores = (log_b + g_pot / entropic)[None, :] - cost
    else:
        scores = log_b[None, :] + (g_pot[None, :] - cost) / entropic
    maxima = jnp.max(scores, axis=1)
    weights = jnp.exp(scores - maxima[:, None])
    panel = jnp.concatenate([fate_panel, jnp.ones((fate_panel.shape[0], 1), jnp.float32)], axis=1)
    product = jnp.dot(
        weights, panel, precision=lax.Precision.HIGHEST, preferred_element_type=jnp.float32
    )
    weighted = product[:, : fate_panel.shape[1]]
    totals = product[:, fate_panel.shape[1]]
    col_size = lax.axis_size("cols")
    rep_size = lax.axis_size("rep")
    fates = fate_panel.shape[1]
    if rep_size == 2 and col_size <= 8:
        block = src_count // (col_size * rep_size)
        rep = lax.axis_index("rep")
        packed = jnp.concatenate([weighted, maxima[:, None], totals[:, None]], axis=-1)
        packed = packed.reshape(col_size, rep_size, block, fates + 2)
        keep = lax.dynamic_index_in_dim(packed, rep, axis=1, keepdims=False)
        send = lax.dynamic_index_in_dim(packed, 1 - rep, axis=1, keepdims=False)
        recv = lax.ppermute(send, "rep", [(0, 1), (1, 0)])
        maxima = jnp.maximum(keep[..., fates], recv[..., fates])
        keep_f = jnp.exp(keep[..., fates] - maxima)
        recv_f = jnp.exp(recv[..., fates] - maxima)
        totals = keep[..., fates + 1] * keep_f + recv[..., fates + 1] * recv_f
        weighted = keep[..., :fates] * keep_f[..., None] + recv[..., :fates] * recv_f[..., None]
        maxima, totals, weighted = lse_scatter_exchange(maxima, totals, weighted, "cols")
        fate_rows = weighted / totals[:, None]
    elif is_pow2(col_size) and is_pow2(rep_size):
        col_bits = col_size.bit_length() - 1
        rep_bits = rep_size.bit_length() - 1
        lead = (2,) * (col_bits + rep_bits)
        block = src_count // (col_size * rep_size)
        maxima = maxima.reshape(lead + (block,))
        totals = totals.reshape(lead + (block,))
        weighted = weighted.reshape(lead + (block, fates))
        order = [("cols", 1 << b) for b in range(col_bits - 1, -1, -1)]
        order += [("rep", 1 << b) for b in range(rep_bits - 1, -1, -1)]
        plan = list(range(len(order) - 1, col_bits - 1, -1)) + list(range(col_bits - 1, -1, -1))
        perm_dims = plan + list(range(len(order), len(order) + 1))
        maxima = jnp.transpose(maxima, perm_dims)
        totals = jnp.transpose(totals, perm_dims)
        weighted = jnp.transpose(weighted, perm_dims + [len(order) + 1])
        maxima, totals, weighted = lse_halving(
            maxima, totals, weighted, [order[d] for d in plan]
        )
        fate_rows = weighted / totals[:, None]
    else:
        whole_peak = lax.pmax(maxima, ("cols", "rep"))
        factor = jnp.exp(maxima - whole_peak)
        part_weighted, part_total = (
            lax.psum_scatter(
                weighted * factor[:, None], ("cols", "rep"), scatter_dimension=0, tiled=True
            ),
            lax.psum_scatter(totals * factor, ("cols", "rep"), scatter_dimension=0, tiled=True),
        )
        fate_rows = part_weighted / part_total[:, None]
    return (g_pot, fate_rows)


ROW_AXES = (("rep",), ("cols",))


def row_reduce(maxima, totals):
    for axes in ROW_AXES:
        if len(axes) == 1 and lax.axis_size(axes[0]) == 2:
            maxima, totals = lse_allreduce(maxima, totals, axes)
        else:
            maxima, totals = lse_exchange(maxima, totals, axes)
    return maxima, totals


def body(sources, source_mass, targets, target_mass, fate_panel):
    row_count = lax.axis_size("rows")
    if row_count != 2 or lax.axis_size("cols") > 8:
        return body_split(sources, source_mass, targets, target_mass, fate_panel)
    src_count = sources.shape[0]
    tgt_count = targets.shape[0]
    row = lax.axis_index("rows")
    dim = sources.shape[1]
    flat = src_count * dim
    lanes = 128
    mine = jnp.concatenate(
        [sources.reshape(flat // lanes, lanes), source_mass.reshape(src_count // lanes, lanes)]
    )
    theirs = lax.ppermute(mine, "rows", [(0, 1), (1, 0)])
    all_sources = src_count * row_count
    all_targets = tgt_count * lax.axis_size(("cols", "rep"))
    log_b = jnp.log(target_mass / all_targets)
    tgt_sq = jnp.sum(targets * targets, axis=1)

    def scaled_cost(src):
        src_sq = jnp.sum(src * src, axis=1)
        return pair_cost(src, src_sq, targets, tgt_sq) / entropic

    scaled_mine = scaled_cost(sources)
    log_a_mine = jnp.log(source_mass / all_sources)
    g_pot = jnp.zeros((tgt_count,), jnp.float32)
    scores = (log_b + g_pot / entropic)[None, :] - scaled_mine
    maxima = jnp.max(scores, axis=1)
    totals = jnp.sum(jnp.exp(scores - maxima[:, None]), axis=1)
    maxima, totals = row_reduce(maxima, totals)
    f_mine = -relaxed * entropic * (maxima + jnp.log(totals))
    scores = (log_a_mine + f_mine / entropic)[:, None] - scaled_mine
    maxima = jnp.max(scores, axis=0)
    totals = jnp.sum(jnp.exp(scores - maxima[None, :]), axis=0)
    maxima, totals = lse_allreduce(maxima, totals, ("rows",))
    g_pot = -relaxed * entropic * (maxima + jnp.log(totals))

    lead = row == 0
    their_src = theirs[: flat // lanes].reshape(src_count, dim)
    their_mass = theirs[flat // lanes :].reshape(src_count)
    all_src = jnp.concatenate(
        [jnp.where(lead, sources, their_src), jnp.where(lead, their_src, sources)]
    )
    all_mass = jnp.concatenate(
        [jnp.where(lead, source_mass, their_mass), jnp.where(lead, their_mass, source_mass)]
    )
    log_a = jnp.log(all_mass / all_sources)
    scaled = with_layout_constraint(scaled_cost(all_src), Layout(major_to_minor=(1, 0)))
    scaled, log_a = lax.optimization_barrier((scaled, log_a))

    for _ in range(1, ITERS):
        scores = (log_b + g_pot / entropic)[None, :] - scaled
        maxima = jnp.max(scores, axis=1)
        totals = jnp.sum(jnp.exp(scores - maxima[:, None]), axis=1)
        maxima, totals = row_reduce(maxima, totals)
        f_all = -relaxed * entropic * (maxima + jnp.log(totals))

        scores = (log_a + f_all / entropic)[:, None] - scaled
        maxima = jnp.max(scores, axis=0)
        totals = jnp.sum(jnp.exp(scores - maxima[None, :]), axis=0)
        g_pot = -relaxed * entropic * (maxima + jnp.log(totals))

    f_pot = lax.dynamic_slice_in_dim(f_all, row * src_count, src_count)
    return (f_pot,) + fate_pullback(scaled_mine, log_b, g_pot, fate_panel, scaled=True)


def solution(mesh):
    in_specs = (
        P(("parts", "rows"), None),
        P(("parts", "rows")),
        P(("parts", "cols", "rep"), None),
        P(("parts", "cols", "rep")),
        P(("parts", "cols", "rep"), None),
    )
    out_specs = (
        P(("parts", "rows")),
        P(("parts", "cols", "rep")),
        P(("parts", "rows", "cols", "rep"), None),
    )

    return jax.shard_map(body, mesh=mesh, in_specs=in_specs, out_specs=out_specs, check_vma=False)
```

```python
import jax
import jax.numpy as jnp
from jax import lax
from jax.experimental.layout import Layout, with_layout_constraint
from jax.sharding import PartitionSpec as P

ITERS = 8


entropic = 0.1
relaxed = 1.0 / 1.1


def pair_cost(lhs_rows, lhs_sq, rhs_rows, rhs_sq):
    products = lax.dot_general(
        lhs_rows,
        rhs_rows,
        (((1,), (1,)), ((), ())),
        precision=lax.Precision.HIGHEST,
        preferred_element_type=jnp.float32,
    )
    return (lhs_sq[:, None] + rhs_sq[None, :] - 2.0 * products) / lhs_rows.shape[1]


def is_pow2(n):
    return n > 0 and (n & (n - 1)) == 0


def merge(m_one, s_one, m_two, s_two):
    top = jnp.maximum(m_one, m_two)
    return top, s_one * jnp.exp(m_one - top) + s_two * jnp.exp(m_two - top)


def lse_allreduce(maxima, totals, axes):
    if not all(is_pow2(lax.axis_size(name)) for name in axes):
        peak = lax.pmax(maxima, axes)
        return peak, lax.psum(totals * jnp.exp(maxima - peak), axes)
    for name in axes:
        size = lax.axis_size(name)
        index = lax.axis_index(name)
        step = 1
        while step < size:
            perm = [(i, i ^ step) for i in range(size)]
            other = lax.ppermute(jnp.stack([maxima, totals]), name, perm)
            other_m, other_s = other[0], other[1]
            low = (index & step) == 0
            lo_m = jnp.where(low, maxima, other_m)
            hi_m = jnp.where(low, other_m, maxima)
            lo_s = jnp.where(low, totals, other_s)
            hi_s = jnp.where(low, other_s, totals)
            maxima, totals = merge(lo_m, lo_s, hi_m, hi_s)
            step *= 2
    return maxima, totals


def lse_exchange(maxima, totals, axes):
    size = lax.axis_size(axes)
    index = lax.axis_index(axes)
    payload = jnp.stack([maxima, totals])
    received = [payload]
    for mask in range(1, size):
        if is_pow2(size):
            perm = [(i, i ^ mask) for i in range(size)]
        else:
            perm = [(i, (i + mask) % size) for i in range(size)]
        received.append(lax.ppermute(payload, axes, perm))
    received = jnp.stack(received)
    if is_pow2(size):
        slots = [index ^ rank for rank in range(size)]
    else:
        slots = [(index - rank) % size for rank in range(size)]
    ordered = [lax.dynamic_index_in_dim(received, slot, axis=0, keepdims=False) for slot in slots]
    peak = ordered[0][0]
    for item in ordered[1:]:
        peak = jnp.maximum(peak, item[0])
    whole = ordered[0][1] * jnp.exp(ordered[0][0] - peak)
    for item in ordered[1:]:
        whole = whole + item[1] * jnp.exp(item[0] - peak)
    return peak, whole


def lse_halving(maxima, totals, weighted, dims):
    for name, step in dims:
        size = lax.axis_size(name)
        perm = [(i, i ^ step) for i in range(size)]
        high = (lax.axis_index(name) & step) != 0

        def split(x):
            lower = lax.index_in_dim(x, 0, axis=0, keepdims=False)
            upper = lax.index_in_dim(x, 1, axis=0, keepdims=False)
            return jnp.where(high, upper, lower), jnp.where(high, lower, upper)

        keep_m, send_m = split(maxima)
        keep_s, send_s = split(totals)
        keep_w, send_w = split(weighted)
        packed = jnp.concatenate([send_w, send_m[..., None], send_s[..., None]], axis=-1)
        packed = lax.ppermute(packed, name, perm)
        fates = weighted.shape[-1]
        recv_w, recv_m, recv_s = packed[..., :fates], packed[..., fates], packed[..., fates + 1]
        top = jnp.maximum(keep_m, recv_m)
        keep_f = jnp.exp(keep_m - top)
        recv_f = jnp.exp(recv_m - top)
        maxima = top
        totals = keep_s * keep_f + recv_s * recv_f
        weighted = keep_w * keep_f[..., None] + recv_w * recv_f[..., None]
    return maxima, totals, weighted


def body_split(sources, source_mass, targets, target_mass, fate_panel):
    src_count = sources.shape[0]
    tgt_count = targets.shape[0]
    all_sources = src_count * lax.axis_size("rows")
    all_targets = tgt_count * lax.axis_size(("cols", "rep"))
    log_a = jnp.log(source_mass / all_sources)
    log_b = jnp.log(target_mass / all_targets)
    src_sq = jnp.sum(sources * sources, axis=1)
    tgt_sq = jnp.sum(targets * targets, axis=1)
    cost = pair_cost(sources, src_sq, targets, tgt_sq)

    g_pot = jnp.zeros((tgt_count,), jnp.float32)
    f_pot = jnp.zeros((src_count,), jnp.float32)
    for _ in range(ITERS):
        scores = log_b[None, :] + (g_pot[None, :] - cost) / entropic
        maxima = jnp.max(scores, axis=1)
        totals = jnp.sum(jnp.exp(scores - maxima[:, None]), axis=1)
        peak, whole = lse_allreduce(maxima, totals, ("rep", "cols"))
        f_pot = -relaxed * entropic * (peak + jnp.log(whole))

        scores = log_a[:, None] + (f_pot[:, None] - cost) / entropic
        maxima = jnp.max(scores, axis=0)
        totals = jnp.sum(jnp.exp(scores - maxima[None, :]), axis=0)
        peak, whole = lse_allreduce(maxima, totals, ("rows",))
        g_pot = -relaxed * entropic * (peak + jnp.log(whole))

    return (f_pot,) + fate_pullback(cost, log_b, g_pot, fate_panel)


def lse_scatter_exchange(maxima, totals, weighted, name):
    size = lax.axis_size(name)
    index = lax.axis_index(name)
    fates = weighted.shape[-1]
    packed = jnp.concatenate([weighted, maxima[..., None], totals[..., None]], axis=-1)
    parts = [lax.dynamic_index_in_dim(packed, index, axis=0, keepdims=False)]
    for shift in range(1, size):
        if is_pow2(size):
            perm = [(i, i ^ shift) for i in range(size)]
            owner = index ^ shift
        else:
            perm = [(i, (i + shift) % size) for i in range(size)]
            owner = (index + shift) % size
        send = lax.dynamic_index_in_dim(packed, owner, axis=0, keepdims=False)
        parts.append(lax.ppermute(send, name, perm))
    top = parts[0][..., fates]
    for part in parts[1:]:
        top = jnp.maximum(top, part[..., fates])
    totals = None
    weighted = None
    for part in parts:
        factor = jnp.exp(part[..., fates] - top)
        add_s = part[..., fates + 1] * factor
        add_w = part[..., :fates] * factor[..., None]
        totals = add_s if totals is None else totals + add_s
        weighted = add_w if weighted is None else weighted + add_w
    return top, totals, weighted


def fate_pullback(cost, log_b, g_pot, fate_panel, scaled=False):
    src_count = cost.shape[0]
    if scaled:
        scores = (log_b + g_pot / entropic)[None, :] - cost
    else:
        scores = log_b[None, :] + (g_pot[None, :] - cost) / entropic
    maxima = jnp.max(scores, axis=1)
    weights = jnp.exp(scores - maxima[:, None])
    panel = jnp.concatenate([fate_panel, jnp.ones((fate_panel.shape[0], 1), jnp.float32)], axis=1)
    product = jnp.dot(
        weights, panel, precision=lax.Precision.HIGHEST, preferred_element_type=jnp.float32
    )
    weighted = product[:, : fate_panel.shape[1]]
    totals = product[:, fate_panel.shape[1]]
    col_size = lax.axis_size("cols")
    rep_size = lax.axis_size("rep")
    fates = fate_panel.shape[1]
    if rep_size == 2 and col_size <= 8:
        block = src_count // (col_size * rep_size)
        rep = lax.axis_index("rep")
        packed = jnp.concatenate([product, maxima[:, None]], axis=-1)
        packed = packed.reshape(col_size, rep_size, block, fates + 2)
        keep = lax.dynamic_index_in_dim(packed, rep, axis=1, keepdims=False)
        send = lax.dynamic_index_in_dim(packed, 1 - rep, axis=1, keepdims=False)
        recv = lax.ppermute(send, "rep", [(0, 1), (1, 0)])
        maxima = jnp.maximum(keep[..., fates + 1], recv[..., fates + 1])
        keep_f = jnp.exp(keep[..., fates + 1] - maxima)
        recv_f = jnp.exp(recv[..., fates + 1] - maxima)
        totals = keep[..., fates] * keep_f + recv[..., fates] * recv_f
        weighted = keep[..., :fates] * keep_f[..., None] + recv[..., :fates] * recv_f[..., None]
        maxima, totals, weighted = lse_scatter_exchange(maxima, totals, weighted, "cols")
        fate_rows = weighted / totals[:, None]
    elif is_pow2(col_size) and is_pow2(rep_size):
        col_bits = col_size.bit_length() - 1
        rep_bits = rep_size.bit_length() - 1
        lead = (2,) * (col_bits + rep_bits)
        block = src_count // (col_size * rep_size)
        maxima = maxima.reshape(lead + (block,))
        totals = totals.reshape(lead + (block,))
        weighted = weighted.reshape(lead + (block, fates))
        order = [("cols", 1 << b) for b in range(col_bits - 1, -1, -1)]
        order += [("rep", 1 << b) for b in range(rep_bits - 1, -1, -1)]
        plan = list(range(len(order) - 1, col_bits - 1, -1)) + list(range(col_bits - 1, -1, -1))
        perm_dims = plan + list(range(len(order), len(order) + 1))
        maxima = jnp.transpose(maxima, perm_dims)
        totals = jnp.transpose(totals, perm_dims)
        weighted = jnp.transpose(weighted, perm_dims + [len(order) + 1])
        maxima, totals, weighted = lse_halving(
            maxima, totals, weighted, [order[d] for d in plan]
        )
        fate_rows = weighted / totals[:, None]
    else:
        whole_peak = lax.pmax(maxima, ("cols", "rep"))
        factor = jnp.exp(maxima - whole_peak)
        part_weighted, part_total = (
            lax.psum_scatter(
                weighted * factor[:, None], ("cols", "rep"), scatter_dimension=0, tiled=True
            ),
            lax.psum_scatter(totals * factor, ("cols", "rep"), scatter_dimension=0, tiled=True),
        )
        fate_rows = part_weighted / part_total[:, None]
    return (g_pot, fate_rows)


ROW_AXES = (("rep",), ("cols",))


def row_reduce(maxima, totals):
    for axes in ROW_AXES:
        if len(axes) == 1 and lax.axis_size(axes[0]) == 2:
            maxima, totals = lse_allreduce(maxima, totals, axes)
        else:
            maxima, totals = lse_exchange(maxima, totals, axes)
    return maxima, totals


def body(sources, source_mass, targets, target_mass, fate_panel):
    row_count = lax.axis_size("rows")
    if row_count != 2 or lax.axis_size("cols") > 8:
        return body_split(sources, source_mass, targets, target_mass, fate_panel)
    src_count = sources.shape[0]
    tgt_count = targets.shape[0]
    row = lax.axis_index("rows")
    dim = sources.shape[1]
    flat = src_count * dim
    lanes = 128
    mine = jnp.concatenate(
        [sources.reshape(flat // lanes, lanes), source_mass.reshape(src_count // lanes, lanes)]
    )
    theirs = lax.ppermute(mine, "rows", [(0, 1), (1, 0)])
    all_sources = src_count * row_count
    all_targets = tgt_count * lax.axis_size(("cols", "rep"))
    log_b = jnp.log(target_mass / all_targets)
    tgt_sq = jnp.sum(targets * targets, axis=1)

    def scaled_cost(src):
        src_sq = jnp.sum(src * src, axis=1)
        return pair_cost(src, src_sq, targets, tgt_sq) / entropic

    scaled_mine = scaled_cost(sources)
    log_a_mine = jnp.log(source_mass / all_sources)
    g_pot = jnp.zeros((tgt_count,), jnp.float32)
    scores = (log_b + g_pot / entropic)[None, :] - scaled_mine
    maxima = jnp.max(scores, axis=1)
    totals = jnp.sum(jnp.exp(scores - maxima[:, None]), axis=1)
    maxima, totals = row_reduce(maxima, totals)
    f_mine = -relaxed * entropic * (maxima + jnp.log(totals))
    scores = (log_a_mine + f_mine / entropic)[:, None] - scaled_mine
    maxima = jnp.max(scores, axis=0)
    totals = jnp.sum(jnp.exp(scores - maxima[None, :]), axis=0)
    maxima, totals = lse_allreduce(maxima, totals, ("rows",))
    g_pot = -relaxed * entropic * (maxima + jnp.log(totals))

    lead = row == 0
    their_src = theirs[: flat // lanes].reshape(src_count, dim)
    their_mass = theirs[flat // lanes :].reshape(src_count)
    all_src = jnp.concatenate(
        [jnp.where(lead, sources, their_src), jnp.where(lead, their_src, sources)]
    )
    all_mass = jnp.concatenate(
        [jnp.where(lead, source_mass, their_mass), jnp.where(lead, their_mass, source_mass)]
    )
    log_a = jnp.log(all_mass / all_sources)
    scaled = with_layout_constraint(scaled_cost(all_src), Layout(major_to_minor=(1, 0)))
    scaled, log_a = lax.optimization_barrier((scaled, log_a))

    for _ in range(1, ITERS):
        scores = (log_b + g_pot / entropic)[None, :] - scaled
        maxima = jnp.max(scores, axis=1)
        totals = jnp.sum(jnp.exp(scores - maxima[:, None]), axis=1)
        maxima, totals = row_reduce(maxima, totals)
        f_all = -relaxed * entropic * (maxima + jnp.log(totals))

        scores = (log_a + f_all / entropic)[:, None] - scaled
        maxima = jnp.max(scores, axis=0)
        totals = jnp.sum(jnp.exp(scores - maxima[None, :]), axis=0)
        g_pot = -relaxed * entropic * (maxima + jnp.log(totals))

    f_pot = lax.dynamic_slice_in_dim(f_all, row * src_count, src_count)
    return (f_pot,) + fate_pullback(scaled_mine, log_b, g_pot, fate_panel, scaled=True)


def solution(mesh):
    in_specs = (
        P(("parts", "rows"), None),
        P(("parts", "rows")),
        P(("parts", "cols", "rep"), None),
        P(("parts", "cols", "rep")),
        P(("parts", "cols", "rep"), None),
    )
    out_specs = (
        P(("parts", "rows")),
        P(("parts", "cols", "rep")),
        P(("parts", "rows", "cols", "rep"), None),
    )

    return jax.shard_map(body, mesh=mesh, in_specs=in_specs, out_specs=out_specs, check_vma=False)
```
